128 devices in a mesh: grp: 8 (over x, core), blk: 16 (over y, z).
Axes of the slice: x: 4, y: 4, z: 4, core: 2. Of those that a mesh axis runs over, the one named last changes fastest.
Arguments:
- features: bfloat16 [8, 16, 4096, 256], P('grp', 'blk'), may hold values from -6 to 6
- hub_rows: int32 [8, 16, 32], P('grp', 'blk'), may hold values from 0 to 4095
- hub_adjacency: bfloat16 [8, 16, 4096, 512], P('grp', 'blk'), as said below
- tile_row: int32 [8, 16, 160], P('grp', 'blk'), may hold values from 0 to 31
- tile_col: int32 [8, 16, 160], P('grp', 'blk'), may hold values from 0 to 63
- tile_count: int32 [8, 16], P('grp', 'blk'), may hold values from 26 to 160, as said below
- tile_values: bfloat16 [8, 16, 160, 128, 128], P('grp', 'blk'), may hold values from 0 to 0.049804688
- send_rows: int32 [8, 16, 8, 16, 32], P('grp', 'blk'), may hold values from 0 to 4095
- weight: bfloat16 [256, 256], replicated, may hold values from -0.375 to 0.375
Outputs:
- activations: bfloat16 [8, 16, 4096, 256], P('grp', 'blk')
The draws below stay inside these ranges and needn't reach their ends.
Inputs may be any that keep to these rules, and one draw needn't show every extreme that they name: `tile_count`: some device has exactly 160 live tile slots in every draw. `hub_adjacency`: Non-negative edge weights.
All inputs are finite; a program needn't handle non-finite values.
Results may differ from the reference program's by a relative error of at most 0.0014.
The reference program's roundings to bfloat16 on the way (of `hub_feats`, `received` and `aggregated`) count: a program that leaves them out, or rounds other values in their place, can miss the bound.
Values may be sent and summed in bfloat16 or wider, within the bound.
No kernel may reach another device: no remote copies, remote signals or barrier semaphores. Data moves between devices by JAX's collectives and lax.ppermute only.
A program may use at most 128 MiB of HBM per device.

```python
import jax
import jax.numpy as jnp
from jax import lax

FEAT = 256
ROWS_DEV = 4096
TB = 128
HUB_DEV = 32
SEND = 32
MAXT = 160
HUBS = 512
RECV = 4096
N_GRP = 8
N_BLK = 16


def draw_hub_adjacency(key, part):
    base = jax.random.uniform(key, (N_GRP, N_BLK, ROWS_DEV, HUBS), jnp.float32)
    factor = (3.0 / HUBS) ** 0.5
    return (base * factor).astype(jnp.bfloat16)


def draw_tile_count(key, part):
    total = N_GRP * N_BLK
    divisor = jax.random.randint(key, (total,), 1, 7)
    counts = MAXT // divisor
    busiest = jax.random.randint(jax.random.fold_in(key, 3), (), 0, total)
    counts = jnp.where(jnp.arange(total) == busiest, MAXT, counts)
    return counts.reshape(N_GRP, N_BLK).astype(jnp.int32)


def place_ends(values, key, smallest, largest):
    longest = values.shape.index(max(values.shape))
    spots = []
    for shift in (0, 1):
        where = [jax.random.randint(jax.random.fold_in(key, axis), (), 0, length) for axis, length in enumerate(values.shape)]
        where[longest] = (where[longest] + shift) % values.shape[longest]
        spots.append(tuple(where))
    return values.at[spots[0]].set(smallest).at[spots[1]].set(largest)


def steps_of(own_key, extent, cuts, least, largest):
    def one(axis_at, parts):
        heights = jax.random.uniform(jax.random.fold_in(jax.random.fold_in(own_key, 6), axis_at), (parts,), jnp.float32, least / len(cuts), largest / len(cuts))
        return jnp.repeat(jnp.exp(heights), extent[axis_at] // parts).reshape((-1,) + (1,) * (len(extent) - axis_at - 1))

    gain = one(*cuts[0])
    for cut in cuts[1:]:
        gain = gain * one(*cut)
    return gain


def scatter_about(key, dims, scale, most, shards=(), kind=jnp.bfloat16):
    values = scale * jax.random.normal(key, dims, jnp.float32)
    if shards:
        values = values * steps_of(key, dims, shards, -0.22, 0.18)
    return jnp.clip(values, -most, most).astype(kind)


def setup_inputs(seed: int = 0) -> dict:
    arg_keys = jax.random.split(jax.random.key(seed), 10)
    return {
        "features": scatter_about(arg_keys[0], (N_GRP, N_BLK, ROWS_DEV, FEAT), 1.0, 6.0, ((0, 8), (1, 16))),
        "hub_rows": place_ends(jax.random.randint(arg_keys[1], (N_GRP, N_BLK, HUB_DEV), 0, ROWS_DEV), jax.random.fold_in(arg_keys[1], 1), 0, ROWS_DEV - 1).astype(jnp.int32),
        "hub_adjacency": draw_hub_adjacency(jax.random.fold_in(arg_keys[9], 71), 0),
        "tile_row": place_ends(jax.random.randint(arg_keys[3], (N_GRP, N_BLK, MAXT), 0, ROWS_DEV // TB), jax.random.fold_in(arg_keys[3], 1), 0, (ROWS_DEV // TB) - 1).astype(jnp.int32),
        "tile_col": place_ends(jax.random.randint(arg_keys[4], (N_GRP, N_BLK, MAXT), 0, (ROWS_DEV + RECV) // TB), jax.random.fold_in(arg_keys[4], 1), 0, ((ROWS_DEV + RECV) // TB) - 1).astype(jnp.int32),
        "tile_count": draw_tile_count(jax.random.fold_in(arg_keys[9], 71), 0),
        "tile_values": jnp.clip(0.049804688 * jax.random.uniform(arg_keys[6], (N_GRP, N_BLK, MAXT, TB, TB), jnp.float32) ** steps_of(arg_keys[6], (N_GRP, N_BLK, MAXT, TB, TB), ((0, 8), (1, 16)), -0.2, 0.2), 0.0, 0.049804688).astype(jnp.bfloat16),
        "send_rows": place_ends(jax.random.randint(arg_keys[7], (N_GRP, N_BLK, N_GRP, N_BLK, SEND), 0, ROWS_DEV), jax.random.fold_in(arg_keys[7], 1), 0, ROWS_DEV - 1).astype(jnp.int32),
        "weight": scatter_about(arg_keys[8], (FEAT, FEAT), FEAT ** -0.5, 0.375),
    }


def pick_rows(table, index):
    return table[index]


def reference(features, hub_rows, hub_adjacency, tile_row, tile_col, tile_count, tile_values, send_rows, weight):
    devices = N_GRP * N_BLK
    hub_feats = jax.vmap(jax.vmap(pick_rows))(features, hub_rows.astype(jnp.int32))
    hub_group = hub_feats.reshape(N_GRP, HUBS, FEAT)
    sent = jax.vmap(jax.vmap(pick_rows))(features, send_rows.astype(jnp.int32))
    received = jnp.transpose(sent, (2, 3, 0, 1, 4, 5)).reshape(devices, RECV, FEAT)
    group = (jnp.arange(devices, dtype=jnp.int32) // N_BLK).astype(jnp.int32)

    def one_device(item):
        local, adjacency, incoming, rows, cols, count, values, owner = item
        hub_part = jnp.dot(adjacency, hub_group[owner], preferred_element_type=jnp.float32)
        table = jnp.concatenate([local, incoming], 0).reshape(-1, TB, FEAT)
        picked = table[cols]
        products = jnp.einsum("tij,tjf->tif", values.astype(jnp.float32), picked.astype(jnp.float32))
        valid = (jnp.arange(MAXT, dtype=jnp.int32) < count).astype(jnp.float32)
        summed = jax.ops.segment_sum(products * valid[:, None, None], rows, num_segments=ROWS_DEV // TB)
        aggregated = (hub_part + summed.reshape(ROWS_DEV, FEAT)).astype(jnp.bfloat16)
        mixed = jnp.dot(aggregated, weight, preferred_element_type=jnp.float32)
        return jnp.maximum(mixed, 0.0).astype(jnp.bfloat16)

    items = (features.reshape(devices, ROWS_DEV, FEAT),
             hub_adjacency.reshape(devices, ROWS_DEV, HUBS),
             received,
             tile_row.reshape(devices, MAXT).astype(jnp.int32),
             tile_col.reshape(devices, MAXT).astype(jnp.int32),
             tile_count.reshape(devices).astype(jnp.int32),
             tile_values.reshape(devices, MAXT, TB, TB),
             group)
    result = lax.map(one_device, items)
    return result.reshape(N_GRP, N_BLK, ROWS_DEV, FEAT)
```

```python
import functools

import jax
import jax.numpy as jnp
from jax import lax
from jax.experimental import pallas as pl
from jax.experimental.pallas import tpu as pltpu
from jax.sharding import PartitionSpec as P

TB = 128
SLOTS_PER_STEP = 8


def _tile_body(rows_ref, cols_ref, count_ref, table_ref, vals_ref, acc_ref, *, lo, step):
    s = pl.program_id(0)
    width = table_ref.shape[0] // TB
    count = count_ref[0]
    for j in range(SLOTS_PER_STEP):
        t = s * SLOTS_PER_STEP + j
        c = cols_ref[t] - lo
        live = (t < count) & (c >= 0) & (c < width)

        @pl.when(live)
        def _():
            r0 = pl.multiple_of(rows_ref[t] * TB, TB)
            c0 = pl.multiple_of(c * TB, TB)
            acc_ref[pl.ds(r0, TB), :] += jnp.dot(
                vals_ref[j], table_ref[pl.ds(c0, TB), :], preferred_element_type=jnp.float32
            )


def _local_kernel(rows_ref, cols_ref, count_ref, table_ref, vals_ref, acc_ref):
    @pl.when(pl.program_id(0) == 0)
    def _():
        acc_ref[...] = jnp.zeros_like(acc_ref)

    _tile_body(rows_ref, cols_ref, count_ref, table_ref, vals_ref, acc_ref, lo=0, step=0)


def _remote_kernel(rows_ref, cols_ref, count_ref, table_ref, vals_ref, part_ref, adj_ref, hub_ref,
                   w_ref, out_ref, acc_ref, *, lo):
    s = pl.program_id(0)
    n = acc_ref.shape[0]
    blk = 512

    @pl.when(s == 0)
    def _():
        for i in range(n // blk):
            sl = pl.ds(i * blk, blk)
            acc_ref[sl, :] = part_ref[sl, :] + jnp.dot(
                adj_ref[sl, :], hub_ref[...], preferred_element_type=jnp.float32
            )

    _tile_body(rows_ref, cols_ref, count_ref, table_ref, vals_ref, acc_ref, lo=lo, step=0)

    @pl.when(s == pl.num_programs(0) - 1)
    def _():
        for i in range(n // blk):
            sl = pl.ds(i * blk, blk)
            agg = acc_ref[sl, :].astype(jnp.bfloat16)
            mixed = jnp.dot(agg, w_ref[...], preferred_element_type=jnp.float32)
            out_ref[sl, :] = jnp.maximum(mixed, 0.0).astype(out_ref.dtype)


def _vals_map(s, rows, cols, count):
    last = jnp.maximum(count[0] - 1, 0) // SLOTS_PER_STEP
    return (jnp.minimum(s, last), 0, 0)


def local_tiles(rows, cols, count, table, vals):
    n, width = table.shape
    slots = vals.shape[0]
    steps = slots // SLOTS_PER_STEP
    const = lambda s, r, c, k: (0, 0)
    return pl.pallas_call(
        _local_kernel,
        grid_spec=pltpu.PrefetchScalarGridSpec(
            num_scalar_prefetch=3,
            grid=(steps,),
            in_specs=[
                pl.BlockSpec((n, width), const),
                pl.BlockSpec((SLOTS_PER_STEP, TB, TB), _vals_map),
            ],
            out_specs=pl.BlockSpec((n, width), const),
        ),
        out_shape=jax.ShapeDtypeStruct((n, width), jnp.float32),
    )(rows, cols, count, table, vals)


def remote_tiles(rows, cols, count, table, vals, part, adj, hub, weight, lo):
    n, width = part.shape
    slots = vals.shape[0]
    steps = slots // SLOTS_PER_STEP
    const = lambda s, r, c, k: (0, 0)
    return pl.pallas_call(
        functools.partial(_remote_kernel, lo=lo),
        grid_spec=pltpu.PrefetchScalarGridSpec(
            num_scalar_prefetch=3,
            grid=(steps,),
            in_specs=[
                pl.BlockSpec(table.shape, const),
                pl.BlockSpec((SLOTS_PER_STEP, TB, TB), _vals_map),
                pl.BlockSpec(part.shape, const),
                pl.BlockSpec(adj.shape, const),
                pl.BlockSpec(hub.shape, const),
                pl.BlockSpec(weight.shape, const),
            ],
            out_specs=pl.BlockSpec((n, width), const),
            scratch_shapes=[pltpu.VMEM((n, width), jnp.float32)],
        ),
        out_shape=jax.ShapeDtypeStruct((n, width), jnp.bfloat16),
    )(rows, cols, count, table, vals, part, adj, hub, weight)


def per_device(
    features,
    hub_rows,
    hub_adjacency,
    tile_row,
    tile_col,
    tile_count,
    tile_values,
    send_rows,
    weight,
):
    local = features[0, 0]
    rows = local.shape[0]
    adjacency = hub_adjacency[0, 0]
    hub_block = local[hub_rows[0, 0]]
    listing = send_rows[0, 0]
    outgoing = local[listing.reshape(-1)]
    incoming = lax.all_to_all(outgoing, ("grp", "blk"), split_axis=0, concat_axis=0, tiled=True)
    hub_group = lax.all_gather(hub_block, "blk", axis=0, tiled=True)
    t_rows = tile_row[0, 0]
    t_cols = tile_col[0, 0]
    count = tile_count[0, 0].reshape(1)
    vals = tile_values[0, 0]
    part = local_tiles(t_rows, t_cols, count, local, vals)
    out = remote_tiles(
        t_rows, t_cols, count, incoming, vals, part, adjacency, hub_group, weight, rows // TB
    )
    return out[None, None]


def solution(mesh):
    return jax.shard_map(
        per_device,
        mesh=mesh,
        in_specs=(
            P("grp", "blk", None, None),
            P("grp", "blk", None),
            P("grp", "blk", None, None),
            P("grp", "blk", None),
            P("grp", "blk", None),
            P("grp", "blk"),
            P("grp", "blk", None, None, None),
            P("grp", "blk", None, None, None),
            P(),
        ),
        out_specs=P("grp", "blk", None, None),
        check_vma=False,
    )
```

```python
import functools

import jax
import jax.numpy as jnp
from jax import lax
from jax.experimental import pallas as pl
from jax.experimental.pallas import tpu as pltpu
from jax.sharding import PartitionSpec as P

TB = 128
SLOTS_PER_STEP = 8


def _tile_body(s, rows_ref, cols_ref, count_ref, table_ref, vals_ref, acc_ref, lo):
    width = table_ref.shape[0] // TB
    count = count_ref[0]
    for j in range(SLOTS_PER_STEP):
        t = s * SLOTS_PER_STEP + j
        c = cols_ref[t] - lo
        live = (t < count) & (c >= 0) & (c < width)

        @pl.when(live)
        def _():
            r0 = pl.multiple_of(rows_ref[t] * TB, TB)
            c0 = pl.multiple_of(c * TB, TB)
            acc_ref[pl.ds(r0, TB), :] += jnp.dot(
                vals_ref[j], table_ref[pl.ds(c0, TB), :], preferred_element_type=jnp.float32
            )


def _local_kernel(rows_ref, cols_ref, count_ref, table_ref, vals_ref, adj_ref, hub_ref, acc_ref):
    n = acc_ref.shape[0]
    blk = 512

    @pl.when(pl.program_id(0) == 0)
    def _():
        for i in range(n // blk):
            sl = pl.ds(i * blk, blk)
            acc_ref[sl, :] = jnp.dot(adj_ref[sl, :], hub_ref[...], preferred_element_type=jnp.float32)

    _tile_body(pl.program_id(0), rows_ref, cols_ref, count_ref, table_ref, vals_ref, acc_ref, 0)


def _remote_kernel(rows_ref, cols_ref, count_ref, table_ref, vals_ref, part_ref, w_ref, out_ref,
                   acc_ref, *, lo, tile_steps):
    s = pl.program_id(0)
    blk = out_ref.shape[0]

    @pl.when(s == 0)
    def _():
        acc_ref[...] = jnp.zeros_like(acc_ref)

    @pl.when(s < tile_steps)
    def _():
        _tile_body(s, rows_ref, cols_ref, count_ref, table_ref, vals_ref, acc_ref, lo)

    @pl.when(s >= tile_steps)
    def _():
        r0 = pl.multiple_of((s - tile_steps) * blk, blk)
        agg = (acc_ref[pl.ds(r0, blk), :] + part_ref[...]).astype(jnp.bfloat16)
        mixed = jnp.dot(agg, w_ref[...], preferred_element_type=jnp.float32)
        out_ref[...] = jnp.maximum(mixed, 0.0).astype(out_ref.dtype)


def _vals_map(s, rows, cols, count):
    last = jnp.maximum(count[0] - 1, 0) // SLOTS_PER_STEP
    return (jnp.minimum(s, last), 0, 0)


def local_tiles(rows, cols, count, table, vals, adj, hub):
    n, width = table.shape
    slots = vals.shape[0]
    steps = slots // SLOTS_PER_STEP
    const = lambda s, r, c, k: (0, 0)
    return pl.pallas_call(
        _local_kernel,
        grid_spec=pltpu.PrefetchScalarGridSpec(
            num_scalar_prefetch=3,
            grid=(steps,),
            in_specs=[
                pl.BlockSpec((n, width), const),
                pl.BlockSpec((SLOTS_PER_STEP, TB, TB), _vals_map),
                pl.BlockSpec(adj.shape, const),
                pl.BlockSpec(hub.shape, const),
            ],
            out_specs=pl.BlockSpec((n, width), const),
        ),
        out_shape=jax.ShapeDtypeStruct((n, width), jnp.float32),
    )(rows, cols, count, table, vals, adj, hub)


def remote_tiles(rows, cols, count, table, vals, part, weight, lo):
    n, width = part.shape
    slots = vals.shape[0]
    tile_steps = slots // SLOTS_PER_STEP
    blk = 512
    fin_steps = n // blk
    const = lambda s, r, c, k: (0, 0)
    fin = lambda s, r, c, k: (jnp.maximum(s - tile_steps, 0), 0)
    return pl.pallas_call(
        functools.partial(_remote_kernel, lo=lo, tile_steps=tile_steps),
        grid_spec=pltpu.PrefetchScalarGridSpec(
            num_scalar_prefetch=3,
            grid=(tile_steps + fin_steps,),
            in_specs=[
                pl.BlockSpec(table.shape, const),
                pl.BlockSpec((SLOTS_PER_STEP, TB, TB), _vals_map),
                pl.BlockSpec((blk, width), fin),
                pl.BlockSpec(weight.shape, const),
            ],
            out_specs=pl.BlockSpec((blk, width), fin),
            scratch_shapes=[pltpu.VMEM((n, width), jnp.float32)],
        ),
        out_shape=jax.ShapeDtypeStruct((n, width), jnp.bfloat16),
    )(rows, cols, count, table, vals, part, weight)


def per_device(
    features,
    hub_rows,
    hub_adjacency,
    tile_row,
    tile_col,
    tile_count,
    tile_values,
    send_rows,
    weight,
):
    local = features[0, 0]
    rows = local.shape[0]
    adjacency = hub_adjacency[0, 0]
    hub_block = local[hub_rows[0, 0]]
    hub_group = lax.all_gather(hub_block, "blk", axis=0, tiled=True)
    hub_group, local = lax.optimization_barrier((hub_group, local))
    listing = send_rows[0, 0]
    outgoing = local[listing.reshape(-1)]
    incoming = lax.all_to_all(outgoing, ("grp", "blk"), split_axis=0, concat_axis=0, tiled=True)
    t_rows = tile_row[0, 0]
    t_cols = tile_col[0, 0]
    count = tile_count[0, 0].reshape(1)
    vals = tile_values[0, 0]
    part = local_tiles(t_rows, t_cols, count, local, vals, adjacency, hub_group)
    out = remote_tiles(t_rows, t_cols, count, incoming, vals, part, weight, rows // TB)
    return out[None, None]


def solution(mesh):
    return jax.shard_map(
        per_device,
        mesh=mesh,
        in_specs=(
            P("grp", "blk", None, None),
            P("grp", "blk", None),
            P("grp", "blk", None, None),
            P("grp", "blk", None),
            P("grp", "blk", None),
            P("grp", "blk"),
            P("grp", "blk", None, None, None),
            P("grp", "blk", None, None, None),
            P(),
        ),
        out_specs=P("grp", "blk", None, None),
        check_vma=False,
    )
```

```python
import functools

import jax
import jax.numpy as jnp
from jax import lax
from jax.experimental import pallas as pl
from jax.experimental.pallas import tpu as pltpu
from jax.sharding import PartitionSpec as P

TB = 128
SLOTS_PER_STEP = 32


def _tile_body(s, rows_ref, cols_ref, count_ref, table_ref, vals_ref, acc_ref, lo):
    width = table_ref.shape[0] // TB
    count = count_ref[0]
    for j in range(SLOTS_PER_STEP):
        t = s * SLOTS_PER_STEP + j
        c = cols_ref[t] - lo
        live = (t < count) & (c >= 0) & (c < width)

        @pl.when(live)
        def _():
            r0 = pl.multiple_of(rows_ref[t] * TB, TB)
            c0 = pl.multiple_of(c * TB, TB)
            acc_ref[pl.ds(r0, TB), :] += jnp.dot(
                vals_ref[j], table_ref[pl.ds(c0, TB), :], preferred_element_type=jnp.float32
            )


def _local_kernel(rows_ref, cols_ref, count_ref, table_ref, vals_ref, adj_ref, hub_ref, acc_ref):
    n = acc_ref.shape[0]
    blk = 512

    @pl.when(pl.program_id(0) == 0)
    def _():
        for i in range(n // blk):
            sl = pl.ds(i * blk, blk)
            acc_ref[sl, :] = jnp.dot(adj_ref[sl, :], hub_ref[...], preferred_element_type=jnp.float32)

    _tile_body(pl.program_id(0), rows_ref, cols_ref, count_ref, table_ref, vals_ref, acc_ref, 0)


def _remote_kernel(rows_ref, cols_ref, count_ref, table_ref, vals_ref, part_ref, w_ref, out_ref,
                   acc_ref, *, lo, tile_steps):
    s = pl.program_id(0)
    blk = out_ref.shape[0]

    @pl.when(s == 0)
    def _():
        acc_ref[...] = jnp.zeros_like(acc_ref)

    @pl.when(s < tile_steps)
    def _():
        _tile_body(s, rows_ref, cols_ref, count_ref, table_ref, vals_ref, acc_ref, lo)

    @pl.when(s >= tile_steps)
    def _():
        r0 = pl.multiple_of((s - tile_steps) * blk, blk)
        agg = (acc_ref[pl.ds(r0, blk), :] + part_ref[...]).astype(jnp.bfloat16)
        mixed = jnp.dot(agg, w_ref[...], preferred_element_type=jnp.float32)
        out_ref[...] = jnp.maximum(mixed, 0.0).astype(out_ref.dtype)


def _vals_map(s, rows, cols, count):
    last = jnp.maximum(count[0] - 1, 0) // SLOTS_PER_STEP
    return (jnp.minimum(s, last), 0, 0)


def local_tiles(rows, cols, count, table, vals, adj, hub):
    n, width = table.shape
    slots = vals.shape[0]
    steps = slots // SLOTS_PER_STEP
    const = lambda s, r, c, k: (0, 0)
    return pl.pallas_call(
        _local_kernel,
        grid_spec=pltpu.PrefetchScalarGridSpec(
            num_scalar_prefetch=3,
            grid=(steps,),
            in_specs=[
                pl.BlockSpec((n, width), const),
                pl.BlockSpec((SLOTS_PER_STEP, TB, TB), _vals_map),
                pl.BlockSpec(adj.shape, const),
                pl.BlockSpec(hub.shape, const),
            ],
            out_specs=pl.BlockSpec((n, width), const),
        ),
        out_shape=jax.ShapeDtypeStruct((n, width), jnp.float32),
    )(rows, cols, count, table, vals, adj, hub)


def remote_tiles(rows, cols, count, table, vals, part, weight, lo):
    n, width = part.shape
    slots = vals.shape[0]
    tile_steps = slots // SLOTS_PER_STEP
    blk = 1024
    fin_steps = n // blk
    const = lambda s, r, c, k: (0, 0)
    fin = lambda s, r, c, k: (jnp.maximum(s - tile_steps, 0), 0)
    return pl.pallas_call(
        functools.partial(_remote_kernel, lo=lo, tile_steps=tile_steps),
        grid_spec=pltpu.PrefetchScalarGridSpec(
            num_scalar_prefetch=3,
            grid=(tile_steps + fin_steps,),
            in_specs=[
                pl.BlockSpec(table.shape, const),
                pl.BlockSpec((SLOTS_PER_STEP, TB, TB), _vals_map),
                pl.BlockSpec((blk, width), fin),
                pl.BlockSpec(weight.shape, const),
            ],
            out_specs=pl.BlockSpec((blk, width), fin),
            scratch_shapes=[pltpu.VMEM((n, width), jnp.float32)],
        ),
        out_shape=jax.ShapeDtypeStruct((n, width), jnp.bfloat16),
    )(rows, cols, count, table, vals, part, weight)


def per_device(
    features,
    hub_rows,
    hub_adjacency,
    tile_row,
    tile_col,
    tile_count,
    tile_values,
    send_rows,
    weight,
):
    local = features[0, 0]
    rows = local.shape[0]
    adjacency = hub_adjacency[0, 0]
    hub_block = local[hub_rows[0, 0]]
    n_blk = lax.axis_size("blk")
    me = lax.axis_index("blk")
    slots = jnp.arange(n_blk, dtype=jnp.int32)[:, None, None] == me
    spread = jnp.where(slots, hub_block[None], jnp.zeros_like(hub_block)[None])
    hub_group = lax.psum(spread, "blk").reshape(-1, hub_block.shape[-1])
    listing = send_rows[0, 0]
    outgoing = local[listing.reshape(-1)]
    incoming = lax.all_to_all(outgoing, ("grp", "blk"), split_axis=0, concat_axis=0, tiled=True)
    t_rows = tile_row[0, 0]
    t_cols = tile_col[0, 0]
    count = tile_count[0, 0].reshape(1)
    vals = tile_values[0, 0]
    part = local_tiles(t_rows, t_cols, count, local, vals, adjacency, hub_group)
    out = remote_tiles(t_rows, t_cols, count, incoming, vals, part, weight, rows // TB)
    return out[None, None]


def solution(mesh):
    return jax.shard_map(
        per_device,
        mesh=mesh,
        in_specs=(
            P("grp", "blk", None, None),
            P("grp", "blk", None),
            P("grp", "blk", None, None),
            P("grp", "blk", None),
            P("grp", "blk", None),
            P("grp", "blk"),
            P("grp", "blk", None, None, None),
            P("grp", "blk", None, None, None),
            P(),
        ),
        out_specs=P("grp", "blk", None, None),
        check_vma=False,
    )
```

```python
import functools

import jax
import jax.numpy as jnp
from jax import lax
from jax.experimental import pallas as pl
from jax.experimental.pallas import tpu as pltpu
from jax.sharding import PartitionSpec as P

TB = 128
SLOTS_PER_STEP = 8


def _tile_body(s, rows_ref, cols_ref, count_ref, table_ref, vals_ref, acc_ref, lo):
    width = table_ref.shape[0] // TB
    count = count_ref[0]
    for j in range(SLOTS_PER_STEP):
        t = s * SLOTS_PER_STEP + j
        c = cols_ref[t] - lo
        live = (t < count) & (c >= 0) & (c < width)

        @pl.when(live)
        def _():
            r0 = pl.multiple_of(rows_ref[t] * TB, TB)
            c0 = pl.multiple_of(c * TB, TB)
            acc_ref[pl.ds(r0, TB), :] += jnp.dot(
                vals_ref[j], table_ref[pl.ds(c0, TB), :], preferred_element_type=jnp.float32
            )


def _local_kernel(rows_ref, cols_ref, count_ref, table_ref, vals_ref, adj_ref, hub_ref, acc_ref):
    n = acc_ref.shape[0]
    blk = 512

    @pl.when(pl.program_id(0) == 0)
    def _():
        for i in range(n // blk):
            sl = pl.ds(i * blk, blk)
            acc_ref[sl, :] = jnp.dot(adj_ref[sl, :], hub_ref[...], preferred_element_type=jnp.float32)

    _tile_body(pl.program_id(0), rows_ref, cols_ref, count_ref, table_ref, vals_ref, acc_ref, 0)


def _remote_kernel(rows_ref, cols_ref, count_ref, table_ref, vals_ref, part_ref, w_ref, out_ref,
                   acc_ref, *, lo, tile_steps):
    s = pl.program_id(0)
    blk = out_ref.shape[0]

    @pl.when(s == 0)
    def _():
        acc_ref[...] = jnp.zeros_like(acc_ref)

    @pl.when(s < tile_steps)
    def _():
        _tile_body(s, rows_ref, cols_ref, count_ref, table_ref, vals_ref, acc_ref, lo)

    @pl.when(s >= tile_steps)
    def _():
        r0 = pl.multiple_of((s - tile_steps) * blk, blk)
        agg = (acc_ref[pl.ds(r0, blk), :] + part_ref[...]).astype(jnp.bfloat16)
        mixed = jnp.dot(agg, w_ref[...], preferred_element_type=jnp.float32)
        out_ref[...] = jnp.maximum(mixed, 0.0).astype(out_ref.dtype)


def _vals_map(s, rows, cols, count):
    last = jnp.maximum(count[0] - 1, 0) // SLOTS_PER_STEP
    return (jnp.minimum(s, last), 0, 0)


def local_tiles(rows, cols, count, table, vals, adj, hub):
    n, width = table.shape
    slots = vals.shape[0]
    steps = slots // SLOTS_PER_STEP
    const = lambda s, r, c, k: (0, 0)
    return pl.pallas_call(
        _local_kernel,
        grid_spec=pltpu.PrefetchScalarGridSpec(
            num_scalar_prefetch=3,
            grid=(steps,),
            in_specs=[
                pl.BlockSpec((n, width), const),
                pl.BlockSpec((SLOTS_PER_STEP, TB, TB), _vals_map),
                pl.BlockSpec(adj.shape, const),
                pl.BlockSpec(hub.shape, const),
            ],
            out_specs=pl.BlockSpec((n, width), const),
        ),
        out_shape=jax.ShapeDtypeStruct((n, width), jnp.float32),
    )(rows, cols, count, table, vals, adj, hub)


def remote_tiles(rows, cols, count, table, vals, part, weight, lo):
    n, width = part.shape
    slots = vals.shape[0]
    tile_steps = slots // SLOTS_PER_STEP
    blk = 512
    fin_steps = n // blk
    const = lambda s, r, c, k: (0, 0)
    fin = lambda s, r, c, k: (jnp.maximum(s - tile_steps, 0), 0)
    return pl.pallas_call(
        functools.partial(_remote_kernel, lo=lo, tile_steps=tile_steps),
        grid_spec=pltpu.PrefetchScalarGridSpec(
            num_scalar_prefetch=3,
            grid=(tile_steps + fin_steps,),
            in_specs=[
                pl.BlockSpec(table.shape, const),
                pl.BlockSpec((SLOTS_PER_STEP, TB, TB), _vals_map),
                pl.BlockSpec((blk, width), fin),
                pl.BlockSpec(weight.shape, const),
            ],
            out_specs=pl.BlockSpec((blk, width), fin),
            scratch_shapes=[pltpu.VMEM((n, width), jnp.float32)],
        ),
        out_shape=jax.ShapeDtypeStruct((n, width), jnp.bfloat16),
    )(rows, cols, count, table, vals, part, weight)


def per_device(
    features,
    hub_rows,
    hub_adjacency,
    tile_row,
    tile_col,
    tile_count,
    tile_values,
    send_rows,
    weight,
):
    local = features[0, 0]
    rows = local.shape[0]
    adjacency = hub_adjacency[0, 0]
    hub_block = local[hub_rows[0, 0]]
    n_blk = lax.axis_size("blk")
    copies = jnp.broadcast_to(hub_block[None], (n_blk,) + hub_block.shape)
    hub_group = lax.all_to_all(copies, "blk", split_axis=0, concat_axis=0, tiled=True)
    hub_group = hub_group.reshape(-1, hub_block.shape[-1])
    listing = send_rows[0, 0]
    outgoing = local[listing.reshape(-1)]
    incoming = lax.all_to_all(outgoing, ("grp", "blk"), split_axis=0, concat_axis=0, tiled=True)
    t_rows = tile_row[0, 0]
    t_cols = tile_col[0, 0]
    count = tile_count[0, 0].reshape(1)
    vals = tile_values[0, 0]
    part = local_tiles(t_rows, t_cols, count, local, vals, adjacency, hub_group)
    out = remote_tiles(t_rows, t_cols, count, incoming, vals, part, weight, rows // TB)
    return out[None, None]


def solution(mesh):
    return jax.shard_map(
        per_device,
        mesh=mesh,
        in_specs=(
            P("grp", "blk", None, None),
            P("grp", "blk", None),
            P("grp", "blk", None, None),
            P("grp", "blk", None),
            P("grp", "blk", None),
            P("grp", "blk"),
            P("grp", "blk", None, None, None),
            P("grp", "blk", None, None, None),
            P(),
        ),
        out_specs=P("grp", "blk", None, None),
        check_vma=False,
    )
```

```python
import functools

import jax
import jax.numpy as jnp
from jax import lax
from jax.experimental import pallas as pl
from jax.experimental.pallas import tpu as pltpu
from jax.sharding import PartitionSpec as P

TB = 128


GROUP = 8


def _slot_loop(order_ref, rows_ref, cols_ref, start, n, table_ref, vals_ref, acc_ref, lo):
    width = table_ref.shape[0] // TB

    def body(g, carry):
        for j in range(GROUP):
            p = g * GROUP + j
            t = order_ref[start + jnp.minimum(p, n - 1)]
            c = jnp.clip(cols_ref[t] - lo, 0, width - 1)
            r0 = pl.multiple_of(rows_ref[t] * TB, TB)
            c0 = pl.multiple_of(c * TB, TB)
            prod = jnp.dot(vals_ref[t], table_ref[pl.ds(c0, TB), :], preferred_element_type=jnp.float32)
            acc_ref[pl.ds(r0, TB), :] += jnp.where(p < n, prod, 0.0)
        return carry

    lax.fori_loop(0, (n + GROUP - 1) // GROUP, body, 0)


def _local_kernel(order_ref, rows_ref, cols_ref, counts_ref, table_ref, vals_ref, adj_ref, hub_ref,
                  acc_ref):
    n = acc_ref.shape[0]
    blk = 512
    for i in range(n // blk):
        sl = pl.ds(i * blk, blk)
        acc_ref[sl, :] = jnp.dot(adj_ref[sl, :], hub_ref[...], preferred_element_type=jnp.float32)
    _slot_loop(order_ref, rows_ref, cols_ref, 0, counts_ref[0], table_ref, vals_ref, acc_ref, 0)


def _remote_kernel(order_ref, rows_ref, cols_ref, counts_ref, table_ref, vals_ref, part_ref, w_ref,
                   out_ref, acc_ref, *, lo):
    s = pl.program_id(0)

    @pl.when(s == 0)
    def _():
        acc_ref[...] = jnp.zeros_like(acc_ref)
        _slot_loop(order_ref, rows_ref, cols_ref, counts_ref[0], counts_ref[1], table_ref, vals_ref,
                   acc_ref, lo)

    @pl.when(s > 0)
    def _():
        blk = out_ref.shape[0]
        r0 = pl.multiple_of((s - 1) * blk, blk)
        agg = (acc_ref[pl.ds(r0, blk), :] + part_ref[...]).astype(jnp.bfloat16)
        mixed = jnp.dot(agg, w_ref[...], preferred_element_type=jnp.float32)
        out_ref[...] = jnp.maximum(mixed, 0.0).astype(out_ref.dtype)


def local_tiles(order, rows, cols, counts, table, vals, adj, hub):
    n, width = table.shape
    const2 = lambda s, *_: (0, 0)
    const3 = lambda s, *_: (0, 0, 0)
    return pl.pallas_call(
        _local_kernel,
        grid_spec=pltpu.PrefetchScalarGridSpec(
            num_scalar_prefetch=4,
            grid=(1,),
            in_specs=[
                pl.BlockSpec((n, width), const2),
                pl.BlockSpec(vals.shape, const3),
                pl.BlockSpec(adj.shape, const2),
                pl.BlockSpec(hub.shape, const2),
            ],
            out_specs=pl.BlockSpec((n, width), const2),
        ),
        out_shape=jax.ShapeDtypeStruct((n, width), jnp.float32),
    )(order, rows, cols, counts, table, vals, adj, hub)


def remote_tiles(order, rows, cols, counts, table, vals, part, weight, lo):
    n, width = part.shape
    blk = 1024
    fin_steps = n // blk
    const2 = lambda s, *_: (0, 0)
    const3 = lambda s, *_: (0, 0, 0)
    fin = lambda s, *_: (jnp.maximum(s - 1, 0), 0)
    return pl.pallas_call(
        functools.partial(_remote_kernel, lo=lo),
        grid_spec=pltpu.PrefetchScalarGridSpec(
            num_scalar_prefetch=4,
            grid=(1 + fin_steps,),
            in_specs=[
                pl.BlockSpec(table.shape, const2),
                pl.BlockSpec(vals.shape, const3),
                pl.BlockSpec((blk, width), fin),
                pl.BlockSpec(weight.shape, const2),
            ],
            out_specs=pl.BlockSpec((blk, width), fin),
            scratch_shapes=[pltpu.VMEM((n, width), jnp.float32)],
        ),
        out_shape=jax.ShapeDtypeStruct((n, width), jnp.bfloat16),
    )(order, rows, cols, counts, table, vals, part, weight)


def slot_order(cols, count, width):
    slots = cols.shape[0]
    t = jnp.arange(slots, dtype=jnp.int32)
    live = t < count
    is_a = live & (cols < width)
    is_b = live & (cols >= width)
    dead = ~live
    n_a = jnp.sum(is_a.astype(jnp.int32))
    n_b = jnp.sum(is_b.astype(jnp.int32))
    pos = jnp.where(
        is_a,
        jnp.cumsum(is_a.astype(jnp.int32)) - 1,
        jnp.where(
            is_b,
            n_a + jnp.cumsum(is_b.astype(jnp.int32)) - 1,
            n_a + n_b + jnp.cumsum(dead.astype(jnp.int32)) - 1,
        ),
    )
    order = jnp.sum(jnp.where(pos[None, :] == t[:, None], t[None, :], 0), axis=1).astype(jnp.int32)
    return order, jnp.stack([n_a, n_b]).astype(jnp.int32)


def per_device(
    features,
    hub_rows,
    hub_adjacency,
    tile_row,
    tile_col,
    tile_count,
    tile_values,
    send_rows,
    weight,
):
    local = features[0, 0]
    rows = local.shape[0]
    adjacency = hub_adjacency[0, 0]
    hub_block = local[hub_rows[0, 0]]
    n_blk = lax.axis_size("blk")
    copies = jnp.broadcast_to(hub_block[None], (n_blk,) + hub_block.shape)
    hub_group = lax.all_to_all(copies, "blk", split_axis=0, concat_axis=0, tiled=True)
    hub_group = hub_group.reshape(-1, hub_block.shape[-1])
    listing = send_rows[0, 0]
    outgoing = local[listing.reshape(-1)]
    incoming = lax.all_to_all(outgoing, ("grp", "blk"), split_axis=0, concat_axis=0, tiled=True)
    t_rows = tile_row[0, 0]
    t_cols = tile_col[0, 0]
    vals = tile_values[0, 0]
    order, counts = slot_order(t_cols, tile_count[0, 0], rows // TB)
    part = local_tiles(order, t_rows, t_cols, counts, local, vals, adjacency, hub_group)
    out = remote_tiles(order, t_rows, t_cols, counts, incoming, vals, part, weight, rows // TB)
    return out[None, None]


def solution(mesh):
    return jax.shard_map(
        per_device,
        mesh=mesh,
        in_specs=(
            P("grp", "blk", None, None),
            P("grp", "blk", None),
            P("grp", "blk", None, None),
            P("grp", "blk", None),
            P("grp", "blk", None),
            P("grp", "blk"),
            P("grp", "blk", None, None, None),
            P("grp", "blk", None, None, None),
            P(),
        ),
        out_specs=P("grp", "blk", None, None),
        check_vma=False,
    )
```

```python
import functools

import jax
import jax.numpy as jnp
from jax import lax
from jax.experimental import pallas as pl
from jax.experimental.pallas import tpu as pltpu
from jax.sharding import PartitionSpec as P

TB = 128


GROUP = 8


def _slot_loop(order_ref, rows_ref, cols_ref, start, n, table_ref, vals_ref, acc_ref, lo):
    width = table_ref.shape[0] // TB

    def body(g, carry):
        for j in range(GROUP):
            p = g * GROUP + j
            t = order_ref[start + jnp.minimum(p, n - 1)]
            c = jnp.clip(cols_ref[t] - lo, 0, width - 1)
            r0 = pl.multiple_of(rows_ref[t] * TB, TB)
            c0 = pl.multiple_of(c * TB, TB)
            prod = jnp.dot(vals_ref[t], table_ref[pl.ds(c0, TB), :], preferred_element_type=jnp.float32)
            acc_ref[pl.ds(r0, TB), :] += jnp.where(p < n, prod, 0.0)
        return carry

    lax.fori_loop(0, (n + GROUP - 1) // GROUP, body, 0)


def _local_kernel(order_ref, rows_ref, cols_ref, counts_ref, table_ref, vals_ref, adj_ref, hub_ref,
                  acc_ref):
    n = acc_ref.shape[0]
    blk = 512
    for i in range(n // blk):
        sl = pl.ds(i * blk, blk)
        acc_ref[sl, :] = jnp.dot(adj_ref[sl, :], hub_ref[...], preferred_element_type=jnp.float32)
    _slot_loop(order_ref, rows_ref, cols_ref, 0, counts_ref[0], table_ref, vals_ref, acc_ref, 0)


def _remote_kernel(order_ref, rows_ref, cols_ref, counts_ref, table_ref, vals_ref, part_ref, w_ref,
                   out_ref, acc_ref, *, lo):
    s = pl.program_id(0)

    @pl.when(s == 0)
    def _():
        acc_ref[...] = jnp.zeros_like(acc_ref)
        _slot_loop(order_ref, rows_ref, cols_ref, counts_ref[0], counts_ref[1], table_ref, vals_ref,
                   acc_ref, lo)

    @pl.when(s > 0)
    def _():
        blk = out_ref.shape[0]
        r0 = pl.multiple_of((s - 1) * blk, blk)
        agg = (acc_ref[pl.ds(r0, blk), :] + part_ref[...]).astype(jnp.bfloat16)
        mixed = jnp.dot(agg, w_ref[...], preferred_element_type=jnp.float32)
        out_ref[...] = jnp.maximum(mixed, 0.0).astype(out_ref.dtype)


def local_tiles(order, rows, cols, counts, table, vals, adj, hub):
    n, width = table.shape
    const2 = lambda s, *_: (0, 0)
    const3 = lambda s, *_: (0, 0, 0)
    return pl.pallas_call(
        _local_kernel,
        grid_spec=pltpu.PrefetchScalarGridSpec(
            num_scalar_prefetch=4,
            grid=(1,),
            in_specs=[
                pl.BlockSpec((n, width), const2),
                pl.BlockSpec(vals.shape, const3),
                pl.BlockSpec(adj.shape, const2),
                pl.BlockSpec(hub.shape, const2),
            ],
            out_specs=pl.BlockSpec((n, width), const2),
        ),
        out_shape=jax.ShapeDtypeStruct((n, width), jnp.float32),
    )(order, rows, cols, counts, table, vals, adj, hub)


def remote_tiles(order, rows, cols, counts, table, vals, part, weight, lo):
    n, width = part.shape
    blk = 1024
    fin_steps = n // blk
    const2 = lambda s, *_: (0, 0)
    const3 = lambda s, *_: (0, 0, 0)
    fin = lambda s, *_: (jnp.maximum(s - 1, 0), 0)
    return pl.pallas_call(
        functools.partial(_remote_kernel, lo=lo),
        grid_spec=pltpu.PrefetchScalarGridSpec(
            num_scalar_prefetch=4,
            grid=(1 + fin_steps,),
            in_specs=[
                pl.BlockSpec(table.shape, const2),
                pl.BlockSpec(vals.shape, const3),
                pl.BlockSpec((blk, width), fin),
                pl.BlockSpec(weight.shape, const2),
            ],
            out_specs=pl.BlockSpec((blk, width), fin),
            scratch_shapes=[pltpu.VMEM((n, width), jnp.float32)],
        ),
        out_shape=jax.ShapeDtypeStruct((n, width), jnp.bfloat16),
    )(order, rows, cols, counts, table, vals, part, weight)


def slot_order(cols, count, width):
    slots = cols.shape[0]
    t = jnp.arange(slots, dtype=jnp.int32)
    live = t < count
    is_a = live & (cols < width)
    is_b = live & (cols >= width)
    dead = ~live
    n_a = jnp.sum(is_a.astype(jnp.int32))
    n_b = jnp.sum(is_b.astype(jnp.int32))
    pos = jnp.where(
        is_a,
        jnp.cumsum(is_a.astype(jnp.int32)) - 1,
        jnp.where(
            is_b,
            n_a + jnp.cumsum(is_b.astype(jnp.int32)) - 1,
            n_a + n_b + jnp.cumsum(dead.astype(jnp.int32)) - 1,
        ),
    )
    order = jnp.sum(jnp.where(pos[None, :] == t[:, None], t[None, :], 0), axis=1).astype(jnp.int32)
    return order, jnp.stack([n_a, n_b]).astype(jnp.int32)


def per_device(
    features,
    hub_rows,
    hub_adjacency,
    tile_row,
    tile_col,
    tile_count,
    tile_values,
    send_rows,
    weight,
):
    local = features[0, 0]
    rows = local.shape[0]
    adjacency = hub_adjacency[0, 0]
    hub_block = local[hub_rows[0, 0]]
    n_blk = lax.axis_size("blk")
    me = lax.axis_index("blk")
    mine = jnp.arange(n_blk, dtype=jnp.int32)[:, None, None] == me
    spread = jnp.where(mine, hub_block[None], jnp.zeros_like(hub_block)[None])
    hub_group = lax.psum(spread, "blk").reshape(-1, hub_block.shape[-1])
    listing = send_rows[0, 0]
    outgoing = local[listing.reshape(-1)]
    hub_group, outgoing = lax.optimization_barrier((hub_group, outgoing))
    incoming = lax.all_to_all(outgoing, ("grp", "blk"), split_axis=0, concat_axis=0, tiled=True)
    t_rows = tile_row[0, 0]
    t_cols = tile_col[0, 0]
    vals = tile_values[0, 0]
    order, counts = slot_order(t_cols, tile_count[0, 0], rows // TB)
    part = local_tiles(order, t_rows, t_cols, counts, local, vals, adjacency, hub_group)
    out = remote_tiles(order, t_rows, t_cols, counts, incoming, vals, part, weight, rows // TB)
    return out[None, None]


def solution(mesh):
    return jax.shard_map(
        per_device,
        mesh=mesh,
        in_specs=(
            P("grp", "blk", None, None),
            P("grp", "blk", None),
            P("grp", "blk", None, None),
            P("grp", "blk", None),
            P("grp", "blk", None),
            P("grp", "blk"),
            P("grp", "blk", None, None, None),
            P("grp", "blk", None, None, None),
            P(),
        ),
        out_specs=P("grp", "blk", None, None),
        check_vma=False,
    )
```

```python
import functools

import jax
import jax.numpy as jnp
from jax import lax
from jax.experimental import pallas as pl
from jax.experimental.pallas import tpu as pltpu
from jax.sharding import PartitionSpec as P

TB = 128


GROUP = 8


def _slot_loop(order_ref, rows_ref, cols_ref, start, n, table_ref, vals_ref, acc_ref, lo):
    width = table_ref.shape[0] // TB

    def body(g, carry):
        for j in range(GROUP):
            p = g * GROUP + j
            t = order_ref[start + jnp.minimum(p, n - 1)]
            c = jnp.clip(cols_ref[t] - lo, 0, width - 1)
            r0 = pl.multiple_of(rows_ref[t] * TB, TB)
            c0 = pl.multiple_of(c * TB, TB)
            prod = jnp.dot(vals_ref[t], table_ref[pl.ds(c0, TB), :], preferred_element_type=jnp.float32)
            acc_ref[pl.ds(r0, TB), :] += jnp.where(p < n, prod, 0.0)
        return carry

    lax.fori_loop(0, (n + GROUP - 1) // GROUP, body, 0)


def _local_kernel(order_ref, rows_ref, cols_ref, counts_ref, table_ref, vals_ref, adj_ref, hub_ref,
                  acc_ref):
    n = acc_ref.shape[0]
    blk = 512
    for i in range(n // blk):
        sl = pl.ds(i * blk, blk)
        acc_ref[sl, :] = jnp.dot(adj_ref[sl, :], hub_ref[...], preferred_element_type=jnp.float32)
    _slot_loop(order_ref, rows_ref, cols_ref, 0, counts_ref[0], table_ref, vals_ref, acc_ref, 0)


def _remote_kernel(order_ref, rows_ref, cols_ref, counts_ref, table_ref, vals_ref, part_ref, w_ref,
                   out_ref, acc_ref, *, lo):
    s = pl.program_id(0)

    @pl.when(s == 0)
    def _():
        acc_ref[...] = jnp.zeros_like(acc_ref)
        _slot_loop(order_ref, rows_ref, cols_ref, counts_ref[0], counts_ref[1], table_ref, vals_ref,
                   acc_ref, lo)

    @pl.when(s > 0)
    def _():
        blk = out_ref.shape[0]
        r0 = pl.multiple_of((s - 1) * blk, blk)
        agg = (acc_ref[pl.ds(r0, blk), :] + part_ref[...]).astype(jnp.bfloat16)
        mixed = jnp.dot(agg, w_ref[...], preferred_element_type=jnp.float32)
        out_ref[...] = jnp.maximum(mixed, 0.0).astype(out_ref.dtype)


def local_tiles(order, rows, cols, counts, table, vals, adj, hub):
    n, width = table.shape
    const2 = lambda s, *_: (0, 0)
    const3 = lambda s, *_: (0, 0, 0)
    return pl.pallas_call(
        _local_kernel,
        grid_spec=pltpu.PrefetchScalarGridSpec(
            num_scalar_prefetch=4,
            grid=(1,),
            in_specs=[
                pl.BlockSpec((n, width), const2),
                pl.BlockSpec(vals.shape, const3),
                pl.BlockSpec(adj.shape, const2),
                pl.BlockSpec(hub.shape, const2),
            ],
            out_specs=pl.BlockSpec((n, width), const2),
        ),
        out_shape=jax.ShapeDtypeStruct((n, width), jnp.float32),
    )(order, rows, cols, counts, table, vals, adj, hub)


def remote_tiles(order, rows, cols, counts, table, vals, part, weight, lo):
    n, width = part.shape
    blk = 1024
    fin_steps = n // blk
    const2 = lambda s, *_: (0, 0)
    const3 = lambda s, *_: (0, 0, 0)
    fin = lambda s, *_: (jnp.maximum(s - 1, 0), 0)
    return pl.pallas_call(
        functools.partial(_remote_kernel, lo=lo),
        grid_spec=pltpu.PrefetchScalarGridSpec(
            num_scalar_prefetch=4,
            grid=(1 + fin_steps,),
            in_specs=[
                pl.BlockSpec(table.shape, const2),
                pl.BlockSpec(vals.shape, const3),
                pl.BlockSpec((blk, width), fin),
                pl.BlockSpec(weight.shape, const2),
            ],
            out_specs=pl.BlockSpec((blk, width), fin),
            scratch_shapes=[pltpu.VMEM((n, width), jnp.float32)],
        ),
        out_shape=jax.ShapeDtypeStruct((n, width), jnp.bfloat16),
    )(order, rows, cols, counts, table, vals, part, weight)


def slot_order(cols, count, width):
    slots = cols.shape[0]
    t = jnp.arange(slots, dtype=jnp.int32)
    live = t < count
    is_a = live & (cols < width)
    is_b = live & (cols >= width)
    dead = ~live
    n_a = jnp.sum(is_a.astype(jnp.int32))
    n_b = jnp.sum(is_b.astype(jnp.int32))
    pos = jnp.where(
        is_a,
        jnp.cumsum(is_a.astype(jnp.int32)) - 1,
        jnp.where(
            is_b,
            n_a + jnp.cumsum(is_b.astype(jnp.int32)) - 1,
            n_a + n_b + jnp.cumsum(dead.astype(jnp.int32)) - 1,
        ),
    )
    order = jnp.sum(jnp.where(pos[None, :] == t[:, None], t[None, :], 0), axis=1).astype(jnp.int32)
    return order, jnp.stack([n_a, n_b]).astype(jnp.int32)


def _gather_kernel(send_ref, hub_idx_ref, feat_ref, out_ref, hub_out_ref, src_ref, dst_ref):
    n = feat_ref.shape[0]
    chunk = 512
    for i in range(n // chunk):
        sl = pl.ds(i * chunk, chunk)
        src_ref[sl, :] = feat_ref[sl, :].astype(jnp.float32)

    def body(g, carry):
        base = pl.multiple_of(g * 8, 8)
        rows = [src_ref[pl.ds(send_ref[base + k], 1), :] for k in range(8)]
        dst_ref[pl.ds(base, 8), :] = jnp.concatenate(rows, axis=0)
        return carry

    lax.fori_loop(0, out_ref.shape[0] // 8, body, 0)
    for i in range(out_ref.shape[0] // chunk):
        sl = pl.ds(i * chunk, chunk)
        out_ref[sl, :] = dst_ref[sl, :].astype(out_ref.dtype)
    hub = jnp.concatenate(
        [src_ref[pl.ds(hub_idx_ref[k], 1), :] for k in range(hub_idx_ref.shape[0])], axis=0
    ).astype(hub_out_ref.dtype)
    for j in range(hub_out_ref.shape[0]):
        hub_out_ref[j] = hub


def gather_rows(send_idx, hub_idx, feat, copies):
    n, width = feat.shape
    m = send_idx.shape[0]
    h = hub_idx.shape[0]
    return pl.pallas_call(
        _gather_kernel,
        grid_spec=pltpu.PrefetchScalarGridSpec(
            num_scalar_prefetch=2,
            grid=(1,),
            in_specs=[pl.BlockSpec((n, width), lambda s, *_: (0, 0))],
            out_specs=[
                pl.BlockSpec((m, width), lambda s, *_: (0, 0)),
                pl.BlockSpec((copies, h, width), lambda s, *_: (0, 0, 0)),
            ],
            scratch_shapes=[pltpu.VMEM((n, width), jnp.float32), pltpu.VMEM((m, width), jnp.float32)],
        ),
        out_shape=[
            jax.ShapeDtypeStruct((m, width), feat.dtype),
            jax.ShapeDtypeStruct((copies, h, width), feat.dtype),
        ],
    )(send_idx, hub_idx, feat)


def per_device(
    features,
    hub_rows,
    hub_adjacency,
    tile_row,
    tile_col,
    tile_count,
    tile_values,
    send_rows,
    weight,
):
    local = features[0, 0]
    rows = local.shape[0]
    adjacency = hub_adjacency[0, 0]
    n_blk = lax.axis_size("blk")
    listing = send_rows[0, 0]
    outgoing, copies = gather_rows(listing.reshape(-1), hub_rows[0, 0], local, n_blk)
    hub_group = lax.all_to_all(copies, "blk", split_axis=0, concat_axis=0, tiled=True)
    hub_group = hub_group.reshape(-1, local.shape[-1])
    incoming = lax.all_to_all(outgoing, ("grp", "blk"), split_axis=0, concat_axis=0, tiled=True)
    t_rows = tile_row[0, 0]
    t_cols = tile_col[0, 0]
    vals = tile_values[0, 0]
    order, counts = slot_order(t_cols, tile_count[0, 0], rows // TB)
    part = local_tiles(order, t_rows, t_cols, counts, local, vals, adjacency, hub_group)
    out = remote_tiles(order, t_rows, t_cols, counts, incoming, vals, part, weight, rows // TB)
    return out[None, None]


def solution(mesh):
    return jax.shard_map(
        per_device,
        mesh=mesh,
        in_specs=(
            P("grp", "blk", None, None),
            P("grp", "blk", None),
            P("grp", "blk", None, None),
            P("grp", "blk", None),
            P("grp", "blk", None),
            P("grp", "blk"),
            P("grp", "blk", None, None, None),
            P("grp", "blk", None, None, None),
            P(),
        ),
        out_specs=P("grp", "blk", None, None),
        check_vma=False,
    )
```

```python
import functools

import jax
import jax.numpy as jnp
from jax import lax
from jax.experimental import pallas as pl
from jax.experimental.pallas import tpu as pltpu
from jax.sharding import PartitionSpec as P

TB = 128


GROUP = 8


def _slot_loop(order_ref, rows_ref, cols_ref, start, n, table_ref, vals_ref, acc_ref, lo):
    width = table_ref.shape[0] // TB

    def body(g, carry):
        for j in range(GROUP):
            p = g * GROUP + j
            t = order_ref[start + jnp.minimum(p, n - 1)]
            c = jnp.clip(cols_ref[t] - lo, 0, width - 1)
            r0 = pl.multiple_of(rows_ref[t] * TB, TB)
            c0 = pl.multiple_of(c * TB, TB)
            prod = jnp.dot(vals_ref[t], table_ref[pl.ds(c0, TB), :], preferred_element_type=jnp.float32)
            acc_ref[pl.ds(r0, TB), :] += jnp.where(p < n, prod, 0.0)
        return carry

    lax.fori_loop(0, (n + GROUP - 1) // GROUP, body, 0)


def _local_kernel(order_ref, rows_ref, cols_ref, counts_ref, table_ref, vals_ref, adj_ref, hub_ref,
                  acc_ref):
    n = acc_ref.shape[0]
    blk = 512
    for i in range(n // blk):
        sl = pl.ds(i * blk, blk)
        acc_ref[sl, :] = jnp.dot(adj_ref[sl, :], hub_ref[...], preferred_element_type=jnp.float32)
    _slot_loop(order_ref, rows_ref, cols_ref, 0, counts_ref[0], table_ref, vals_ref, acc_ref, 0)


def _remote_kernel(order_ref, rows_ref, cols_ref, counts_ref, table_ref, vals_ref, part_ref, w_ref,
                   out_ref, acc_ref, *, lo):
    s = pl.program_id(0)

    @pl.when(s == 0)
    def _():
        acc_ref[...] = jnp.zeros_like(acc_ref)
        _slot_loop(order_ref, rows_ref, cols_ref, counts_ref[0], counts_ref[1], table_ref, vals_ref,
                   acc_ref, lo)

    @pl.when(s > 0)
    def _():
        blk = out_ref.shape[0]
        r0 = pl.multiple_of((s - 1) * blk, blk)
        agg = (acc_ref[pl.ds(r0, blk), :] + part_ref[...]).astype(jnp.bfloat16)
        mixed = jnp.dot(agg, w_ref[...], preferred_element_type=jnp.float32)
        out_ref[...] = jnp.maximum(mixed, 0.0).astype(out_ref.dtype)


def local_tiles(order, rows, cols, counts, table, vals, adj, hub):
    n, width = table.shape
    const2 = lambda s, *_: (0, 0)
    const3 = lambda s, *_: (0, 0, 0)
    return pl.pallas_call(
        _local_kernel,
        grid_spec=pltpu.PrefetchScalarGridSpec(
            num_scalar_prefetch=4,
            grid=(1,),
            in_specs=[
                pl.BlockSpec((n, width), const2),
                pl.BlockSpec(vals.shape, const3),
                pl.BlockSpec(adj.shape, const2),
                pl.BlockSpec(hub.shape, const2),
            ],
            out_specs=pl.BlockSpec((n, width), const2),
        ),
        out_shape=jax.ShapeDtypeStruct((n, width), jnp.float32),
    )(order, rows, cols, counts, table, vals, adj, hub)


def remote_tiles(order, rows, cols, counts, table, vals, part, weight, lo):
    n, width = part.shape
    blk = 1024
    fin_steps = n // blk
    const2 = lambda s, *_: (0, 0)
    const3 = lambda s, *_: (0, 0, 0)
    fin = lambda s, *_: (jnp.maximum(s - 1, 0), 0)
    return pl.pallas_call(
        functools.partial(_remote_kernel, lo=lo),
        grid_spec=pltpu.PrefetchScalarGridSpec(
            num_scalar_prefetch=4,
            grid=(1 + fin_steps,),
            in_specs=[
                pl.BlockSpec(table.shape, const2),
                pl.BlockSpec(vals.shape, const3),
                pl.BlockSpec((blk, width), fin),
                pl.BlockSpec(weight.shape, const2),
            ],
            out_specs=pl.BlockSpec((blk, width), fin),
            scratch_shapes=[pltpu.VMEM((n, width), jnp.float32)],
        ),
        out_shape=jax.ShapeDtypeStruct((n, width), jnp.bfloat16),
    )(order, rows, cols, counts, table, vals, part, weight)


def slot_order(cols, count, width):
    slots = cols.shape[0]
    t = jnp.arange(slots, dtype=jnp.int32)
    live = t < count
    is_a = live & (cols < width)
    is_b = live & (cols >= width)
    dead = ~live
    n_a = jnp.sum(is_a.astype(jnp.int32))
    n_b = jnp.sum(is_b.astype(jnp.int32))
    pos = jnp.where(
        is_a,
        jnp.cumsum(is_a.astype(jnp.int32)) - 1,
        jnp.where(
            is_b,
            n_a + jnp.cumsum(is_b.astype(jnp.int32)) - 1,
            n_a + n_b + jnp.cumsum(dead.astype(jnp.int32)) - 1,
        ),
    )
    order = jnp.sum(jnp.where(pos[None, :] == t[:, None], t[None, :], 0), axis=1).astype(jnp.int32)
    return order, jnp.stack([n_a, n_b]).astype(jnp.int32)


def _gather_kernel(send_ref, hub_idx_ref, feat_ref, out_ref, hub_out_ref, src_ref, dst_ref):
    n = feat_ref.shape[0]
    chunk = 512
    for i in range(n // chunk):
        sl = pl.ds(i * chunk, chunk)
        src_ref[sl, :] = feat_ref[sl, :].astype(jnp.float32)

    def body(g, carry):
        base = pl.multiple_of(g * 8, 8)
        rows = [src_ref[pl.ds(send_ref[base + k], 1), :] for k in range(8)]
        dst_ref[pl.ds(base, 8), :] = jnp.concatenate(rows, axis=0)
        return carry

    lax.fori_loop(0, out_ref.shape[0] // 8, body, 0)
    for i in range(out_ref.shape[0] // chunk):
        sl = pl.ds(i * chunk, chunk)
        out_ref[sl, :] = dst_ref[sl, :].astype(out_ref.dtype)
    hub = jnp.concatenate(
        [src_ref[pl.ds(hub_idx_ref[k], 1), :] for k in range(hub_idx_ref.shape[0])], axis=0
    ).astype(hub_out_ref.dtype)
    for j in range(hub_out_ref.shape[0]):
        hub_out_ref[j] = hub


def gather_rows(send_idx, hub_idx, feat, copies):
    n, width = feat.shape
    m = send_idx.shape[0]
    h = hub_idx.shape[0]
    return pl.pallas_call(
        _gather_kernel,
        grid_spec=pltpu.PrefetchScalarGridSpec(
            num_scalar_prefetch=2,
            grid=(1,),
            in_specs=[pl.BlockSpec((n, width), lambda s, *_: (0, 0))],
            out_specs=[
                pl.BlockSpec((m, width), lambda s, *_: (0, 0)),
                pl.BlockSpec((copies, h, width), lambda s, *_: (0, 0, 0)),
            ],
            scratch_shapes=[pltpu.VMEM((n, width), jnp.float32), pltpu.VMEM((m, width), jnp.float32)],
        ),
        out_shape=[
            jax.ShapeDtypeStruct((m, width), feat.dtype),
            jax.ShapeDtypeStruct((copies, h, width), feat.dtype),
        ],
    )(send_idx, hub_idx, feat)


def per_device(
    features,
    hub_rows,
    hub_adjacency,
    tile_row,
    tile_col,
    tile_count,
    tile_values,
    send_rows,
    weight,
):
    local = features[0, 0]
    rows = local.shape[0]
    adjacency = hub_adjacency[0, 0]
    n_blk = lax.axis_size("blk")
    me = lax.axis_index("blk")
    hub_block = local[hub_rows[0, 0]]
    shifted = [hub_block] + [
        lax.ppermute(hub_block, "blk", [(i, (i + k) % n_blk) for i in range(n_blk)])
        for k in range(1, n_blk)
    ]
    stacked = jnp.stack(shifted[::-1], axis=0)
    hub_group = jnp.roll(stacked, me + 1, axis=0).reshape(-1, local.shape[-1])
    listing = send_rows[0, 0]
    outgoing, _ = gather_rows(listing.reshape(-1), hub_rows[0, 0], local, 1)
    incoming = lax.all_to_all(outgoing, ("grp", "blk"), split_axis=0, concat_axis=0, tiled=True)
    t_rows = tile_row[0, 0]
    t_cols = tile_col[0, 0]
    vals = tile_values[0, 0]
    order, counts = slot_order(t_cols, tile_count[0, 0], rows // TB)
    part = local_tiles(order, t_rows, t_cols, counts, local, vals, adjacency, hub_group)
    out = remote_tiles(order, t_rows, t_cols, counts, incoming, vals, part, weight, rows // TB)
    return out[None, None]


def solution(mesh):
    return jax.shard_map(
        per_device,
        mesh=mesh,
        in_specs=(
            P("grp", "blk", None, None),
            P("grp", "blk", None),
            P("grp", "blk", None, None),
            P("grp", "blk", None),
            P("grp", "blk", None),
            P("grp", "blk"),
            P("grp", "blk", None, None, None),
            P("grp", "blk", None, None, None),
            P(),
        ),
        out_specs=P("grp", "blk", None, None),
        check_vma=False,
    )
```

```python
import functools

import jax
import jax.numpy as jnp
from jax import lax
from jax.experimental import pallas as pl
from jax.experimental.pallas import tpu as pltpu
from jax.sharding import PartitionSpec as P

TB = 128


GROUP = 8


def _slot_loop(order_ref, rows_ref, cols_ref, start, n, table_ref, vals_ref, acc_ref, lo):
    width = table_ref.shape[0] // TB

    def body(g, carry):
        for j in range(GROUP):
            p = g * GROUP + j
            t = order_ref[start + jnp.minimum(p, n - 1)]
            c = jnp.clip(cols_ref[t] - lo, 0, width - 1)
            r0 = pl.multiple_of(rows_ref[t] * TB, TB)
            c0 = pl.multiple_of(c * TB, TB)
            prod = jnp.dot(vals_ref[t], table_ref[pl.ds(c0, TB), :], preferred_element_type=jnp.float32)
            acc_ref[pl.ds(r0, TB), :] += jnp.where(p < n, prod, 0.0)
        return carry

    lax.fori_loop(0, (n + GROUP - 1) // GROUP, body, 0)


def _local_kernel(order_ref, rows_ref, cols_ref, counts_ref, table_ref, vals_ref, adj_ref, hub_ref,
                  acc_ref):
    n = acc_ref.shape[0]
    blk = 512
    for i in range(n // blk):
        sl = pl.ds(i * blk, blk)
        acc_ref[sl, :] = jnp.dot(adj_ref[sl, :], hub_ref[...], preferred_element_type=jnp.float32)
    _slot_loop(order_ref, rows_ref, cols_ref, 0, counts_ref[0], table_ref, vals_ref, acc_ref, 0)


def _remote_kernel(order_ref, rows_ref, cols_ref, counts_ref, table_ref, vals_ref, part_ref, w_ref,
                   out_ref, acc_ref, *, lo):
    s = pl.program_id(0)

    @pl.when(s == 0)
    def _():
        acc_ref[...] = jnp.zeros_like(acc_ref)
        _slot_loop(order_ref, rows_ref, cols_ref, counts_ref[0], counts_ref[1], table_ref, vals_ref,
                   acc_ref, lo)

    @pl.when(s > 0)
    def _():
        blk = out_ref.shape[0]
        r0 = pl.multiple_of((s - 1) * blk, blk)
        agg = (acc_ref[pl.ds(r0, blk), :] + part_ref[...]).astype(jnp.bfloat16)
        mixed = jnp.dot(agg, w_ref[...], preferred_element_type=jnp.float32)
        out_ref[...] = jnp.maximum(mixed, 0.0).astype(out_ref.dtype)


def local_tiles(order, rows, cols, counts, table, vals, adj, hub):
    n, width = table.shape
    const2 = lambda s, *_: (0, 0)
    const3 = lambda s, *_: (0, 0, 0)
    return pl.pallas_call(
        _local_kernel,
        grid_spec=pltpu.PrefetchScalarGridSpec(
            num_scalar_prefetch=4,
            grid=(1,),
            in_specs=[
                pl.BlockSpec((n, width), const2),
                pl.BlockSpec(vals.shape, const3),
                pl.BlockSpec(adj.shape, const2),
                pl.BlockSpec(hub.shape, const2),
            ],
            out_specs=pl.BlockSpec((n, width), const2),
        ),
        out_shape=jax.ShapeDtypeStruct((n, width), jnp.float32),
    )(order, rows, cols, counts, table, vals, adj, hub)


def remote_tiles(order, rows, cols, counts, table, vals, part, weight, lo):
    n, width = part.shape
    blk = 1024
    fin_steps = n // blk
    const2 = lambda s, *_: (0, 0)
    const3 = lambda s, *_: (0, 0, 0)
    fin = lambda s, *_: (jnp.maximum(s - 1, 0), 0)
    return pl.pallas_call(
        functools.partial(_remote_kernel, lo=lo),
        grid_spec=pltpu.PrefetchScalarGridSpec(
            num_scalar_prefetch=4,
            grid=(1 + fin_steps,),
            in_specs=[
                pl.BlockSpec(table.shape, const2),
                pl.BlockSpec(vals.shape, const3),
                pl.BlockSpec((blk, width), fin),
                pl.BlockSpec(weight.shape, const2),
            ],
            out_specs=pl.BlockSpec((blk, width), fin),
            scratch_shapes=[pltpu.VMEM((n, width), jnp.float32)],
        ),
        out_shape=jax.ShapeDtypeStruct((n, width), jnp.bfloat16),
    )(order, rows, cols, counts, table, vals, part, weight)


def slot_order(cols, count, width):
    slots = cols.shape[0]
    t = jnp.arange(slots, dtype=jnp.int32)
    live = t < count
    is_a = live & (cols < width)
    is_b = live & (cols >= width)
    dead = ~live
    n_a = jnp.sum(is_a.astype(jnp.int32))
    n_b = jnp.sum(is_b.astype(jnp.int32))
    pos = jnp.where(
        is_a,
        jnp.cumsum(is_a.astype(jnp.int32)) - 1,
        jnp.where(
            is_b,
            n_a + jnp.cumsum(is_b.astype(jnp.int32)) - 1,
            n_a + n_b + jnp.cumsum(dead.astype(jnp.int32)) - 1,
        ),
    )
    order = jnp.sum(jnp.where(pos[None, :] == t[:, None], t[None, :], 0), axis=1).astype(jnp.int32)
    return order, jnp.stack([n_a, n_b]).astype(jnp.int32)


def _gather_kernel(send_ref, feat_ref, out_ref, src_ref, dst_ref):
    n = feat_ref.shape[0]
    chunk = 512
    for i in range(n // chunk):
        sl = pl.ds(i * chunk, chunk)
        src_ref[sl, :] = feat_ref[sl, :].astype(jnp.float32)

    def body(g, carry):
        base = pl.multiple_of(g * 8, 8)
        rows = [src_ref[pl.ds(send_ref[base + k], 1), :] for k in range(8)]
        dst_ref[pl.ds(base, 8), :] = jnp.concatenate(rows, axis=0)
        return carry

    lax.fori_loop(0, out_ref.shape[0] // 8, body, 0)
    for i in range(out_ref.shape[0] // chunk):
        sl = pl.ds(i * chunk, chunk)
        out_ref[sl, :] = dst_ref[sl, :].astype(out_ref.dtype)


def gather_rows(send_idx, feat):
    n, width = feat.shape
    m = send_idx.shape[0]
    return pl.pallas_call(
        _gather_kernel,
        grid_spec=pltpu.PrefetchScalarGridSpec(
            num_scalar_prefetch=1,
            grid=(1,),
            in_specs=[pl.BlockSpec((n, width), lambda s, *_: (0, 0))],
            out_specs=pl.BlockSpec((m, width), lambda s, *_: (0, 0)),
            scratch_shapes=[pltpu.VMEM((n, width), jnp.float32), pltpu.VMEM((m, width), jnp.float32)],
        ),
        out_shape=jax.ShapeDtypeStruct((m, width), feat.dtype),
    )(send_idx, feat)


def per_device(
    features,
    hub_rows,
    hub_adjacency,
    tile_row,
    tile_col,
    tile_count,
    tile_values,
    send_rows,
    weight,
):
    local = features[0, 0]
    rows = local.shape[0]
    adjacency = hub_adjacency[0, 0]
    n_blk = lax.axis_size("blk")
    hub_block = local[hub_rows[0, 0]]
    copies = jnp.broadcast_to(hub_block[None], (n_blk,) + hub_block.shape)
    hub_group = lax.all_to_all(copies, "blk", split_axis=0, concat_axis=0, tiled=True)
    hub_group = hub_group.reshape(-1, local.shape[-1])
    listing = send_rows[0, 0]
    outgoing = gather_rows(listing.reshape(-1), local)
    incoming = lax.all_to_all(outgoing, ("grp", "blk"), split_axis=0, concat_axis=0, tiled=True)
    t_rows = tile_row[0, 0]
    t_cols = tile_col[0, 0]
    vals = tile_values[0, 0]
    order, counts = slot_order(t_cols, tile_count[0, 0], rows // TB)
    part = local_tiles(order, t_rows, t_cols, counts, local, vals, adjacency, hub_group)
    out = remote_tiles(order, t_rows, t_cols, counts, incoming, vals, part, weight, rows // TB)
    return out[None, None]


def solution(mesh):
    return jax.shard_map(
        per_device,
        mesh=mesh,
        in_specs=(
            P("grp", "blk", None, None),
            P("grp", "blk", None),
            P("grp", "blk", None, None),
            P("grp", "blk", None),
            P("grp", "blk", None),
            P("grp", "blk"),
            P("grp", "blk", None, None, None),
            P("grp", "blk", None, None, None),
            P(),
        ),
        out_specs=P("grp", "blk", None, None),
        check_vma=False,
    )
```

```python
import functools

import jax
import jax.numpy as jnp
from jax import lax
from jax.experimental import pallas as pl
from jax.experimental.pallas import tpu as pltpu
from jax.sharding import PartitionSpec as P

TB = 128


GROUP = 8


def _slot_loop(order_ref, rows_ref, cols_ref, start, n, table_ref, vals_ref, acc_ref, lo):
    width = table_ref.shape[0] // TB

    def body(g, carry):
        for j in range(GROUP):
            p = g * GROUP + j
            t = order_ref[start + jnp.minimum(p, n - 1)]
            c = jnp.clip(cols_ref[t] - lo, 0, width - 1)
            r0 = pl.multiple_of(rows_ref[t] * TB, TB)
            c0 = pl.multiple_of(c * TB, TB)
            prod = jnp.dot(vals_ref[t], table_ref[pl.ds(c0, TB), :], preferred_element_type=jnp.float32)
            acc_ref[pl.ds(r0, TB), :] += jnp.where(p < n, prod, 0.0)
        return carry

    lax.fori_loop(0, (n + GROUP - 1) // GROUP, body, 0)


def _local_kernel(order_ref, rows_ref, cols_ref, counts_ref, table_ref, vals_ref, adj_ref, hub_ref,
                  acc_ref):
    n = acc_ref.shape[0]
    blk = 512
    for i in range(n // blk):
        sl = pl.ds(i * blk, blk)
        acc_ref[sl, :] = jnp.dot(adj_ref[sl, :], hub_ref[...], preferred_element_type=jnp.float32)
    _slot_loop(order_ref, rows_ref, cols_ref, 0, counts_ref[0], table_ref, vals_ref, acc_ref, 0)


def _remote_kernel(order_ref, rows_ref, cols_ref, counts_ref, table_ref, vals_ref, part_ref, w_ref,
                   out_ref, acc_ref, *, lo):
    s = pl.program_id(0)

    @pl.when(s == 0)
    def _():
        acc_ref[...] = jnp.zeros_like(acc_ref)
        _slot_loop(order_ref, rows_ref, cols_ref, counts_ref[0], counts_ref[1], table_ref, vals_ref,
                   acc_ref, lo)

    @pl.when(s > 0)
    def _():
        blk = out_ref.shape[0]
        r0 = pl.multiple_of((s - 1) * blk, blk)
        agg = (acc_ref[pl.ds(r0, blk), :] + part_ref[...]).astype(jnp.bfloat16)
        mixed = jnp.dot(agg, w_ref[...], preferred_element_type=jnp.float32)
        out_ref[...] = jnp.maximum(mixed, 0.0).astype(out_ref.dtype)


def local_tiles(order, rows, cols, counts, table, vals, adj, hub):
    n, width = table.shape
    const2 = lambda s, *_: (0, 0)
    const3 = lambda s, *_: (0, 0, 0)
    return pl.pallas_call(
        _local_kernel,
        grid_spec=pltpu.PrefetchScalarGridSpec(
            num_scalar_prefetch=4,
            grid=(1,),
            in_specs=[
                pl.BlockSpec((n, width), const2),
                pl.BlockSpec(vals.shape, const3),
                pl.BlockSpec(adj.shape, const2),
                pl.BlockSpec(hub.shape, const2),
            ],
            out_specs=pl.BlockSpec((n, width), const2),
        ),
        out_shape=jax.ShapeDtypeStruct((n, width), jnp.float32),
    )(order, rows, cols, counts, table, vals, adj, hub)


def remote_tiles(order, rows, cols, counts, table, vals, part, weight, lo):
    n, width = part.shape
    blk = 1024
    fin_steps = n // blk
    const2 = lambda s, *_: (0, 0)
    const3 = lambda s, *_: (0, 0, 0)
    fin = lambda s, *_: (jnp.maximum(s - 1, 0), 0)
    return pl.pallas_call(
        functools.partial(_remote_kernel, lo=lo),
        grid_spec=pltpu.PrefetchScalarGridSpec(
            num_scalar_prefetch=4,
            grid=(1 + fin_steps,),
            in_specs=[
                pl.BlockSpec(table.shape, const2),
                pl.BlockSpec(vals.shape, const3),
                pl.BlockSpec((blk, width), fin),
                pl.BlockSpec(weight.shape, const2),
            ],
            out_specs=pl.BlockSpec((blk, width), fin),
            scratch_shapes=[pltpu.VMEM((n, width), jnp.float32)],
        ),
        out_shape=jax.ShapeDtypeStruct((n, width), jnp.bfloat16),
    )(order, rows, cols, counts, table, vals, part, weight)


def slot_order(cols, count, width):
    slots = cols.shape[0]
    t = jnp.arange(slots, dtype=jnp.int32)
    live = t < count
    is_a = live & (cols < width)
    is_b = live & (cols >= width)
    dead = ~live
    n_a = jnp.sum(is_a.astype(jnp.int32))
    n_b = jnp.sum(is_b.astype(jnp.int32))
    pos = jnp.where(
        is_a,
        jnp.cumsum(is_a.astype(jnp.int32)) - 1,
        jnp.where(
            is_b,
            n_a + jnp.cumsum(is_b.astype(jnp.int32)) - 1,
            n_a + n_b + jnp.cumsum(dead.astype(jnp.int32)) - 1,
        ),
    )
    order = jnp.sum(jnp.where(pos[None, :] == t[:, None], t[None, :], 0), axis=1).astype(jnp.int32)
    return order, jnp.stack([n_a, n_b]).astype(jnp.int32)


def _gather_kernel(send_ref, feat_ref, out_ref, src_ref, dst_ref):
    n = feat_ref.shape[0]
    chunk = 512
    for i in range(n // chunk):
        sl = pl.ds(i * chunk, chunk)
        src_ref[sl, :] = feat_ref[sl, :].astype(jnp.float32)

    def body(g, carry):
        base = pl.multiple_of(g * 16, 16)
        for k in range(16):
            dst_ref[pl.ds(base + k, 1), :] = src_ref[pl.ds(send_ref[base + k], 1), :]
        return carry

    lax.fori_loop(0, out_ref.shape[0] // 16, body, 0)
    for i in range(out_ref.shape[0] // chunk):
        sl = pl.ds(i * chunk, chunk)
        out_ref[sl, :] = dst_ref[sl, :].astype(out_ref.dtype)


def gather_rows(send_idx, feat):
    n, width = feat.shape
    m = send_idx.shape[0]
    return pl.pallas_call(
        _gather_kernel,
        grid_spec=pltpu.PrefetchScalarGridSpec(
            num_scalar_prefetch=1,
            grid=(1,),
            in_specs=[pl.BlockSpec((n, width), lambda s, *_: (0, 0))],
            out_specs=pl.BlockSpec((m, width), lambda s, *_: (0, 0)),
            scratch_shapes=[pltpu.VMEM((n, width), jnp.float32), pltpu.VMEM((m, width), jnp.float32)],
        ),
        out_shape=jax.ShapeDtypeStruct((m, width), feat.dtype),
    )(send_idx, feat)


def per_device(
    features,
    hub_rows,
    hub_adjacency,
    tile_row,
    tile_col,
    tile_count,
    tile_values,
    send_rows,
    weight,
):
    local = features[0, 0]
    rows = local.shape[0]
    adjacency = hub_adjacency[0, 0]
    n_blk = lax.axis_size("blk")
    hub_block = local[hub_rows[0, 0]]
    copies = jnp.broadcast_to(hub_block[None], (n_blk,) + hub_block.shape)
    hub_group = lax.all_to_all(copies, "blk", split_axis=0, concat_axis=0, tiled=True)
    hub_group = hub_group.reshape(-1, local.shape[-1])
    listing = send_rows[0, 0]
    outgoing = gather_rows(listing.reshape(-1), local)
    incoming = lax.all_to_all(outgoing, ("grp", "blk"), split_axis=0, concat_axis=0, tiled=True)
    t_rows = tile_row[0, 0]
    t_cols = tile_col[0, 0]
    vals = tile_values[0, 0]
    order, counts = slot_order(t_cols, tile_count[0, 0], rows // TB)
    part = local_tiles(order, t_rows, t_cols, counts, local, vals, adjacency, hub_group)
    out = remote_tiles(order, t_rows, t_cols, counts, incoming, vals, part, weight, rows // TB)
    return out[None, None]


def solution(mesh):
    return jax.shard_map(
        per_device,
        mesh=mesh,
        in_specs=(
            P("grp", "blk", None, None),
            P("grp", "blk", None),
            P("grp", "blk", None, None),
            P("grp", "blk", None),
            P("grp", "blk", None),
            P("grp", "blk"),
            P("grp", "blk", None, None, None),
            P("grp", "blk", None, None, None),
            P(),
        ),
        out_specs=P("grp", "blk", None, None),
        check_vma=False,
    )
```

```python
import functools

import jax
import jax.numpy as jnp
from jax import lax
from jax.experimental import pallas as pl
from jax.experimental.pallas import tpu as pltpu
from jax.sharding import PartitionSpec as P

TB = 128


GROUP = 8


def _slot_loop(order_ref, rows_ref, cols_ref, start, n, table_ref, vals_ref, acc_ref, lo):
    width = table_ref.shape[0] // TB

    def body(g, carry):
        for j in range(GROUP):
            p = g * GROUP + j
            t = order_ref[start + jnp.minimum(p, n - 1)]
            c = jnp.clip(cols_ref[t] - lo, 0, width - 1)
            r0 = pl.multiple_of(rows_ref[t] * TB, TB)
            c0 = pl.multiple_of(c * TB, TB)
            prod = jnp.dot(vals_ref[t], table_ref[pl.ds(c0, TB), :], preferred_element_type=jnp.float32)
            acc_ref[pl.ds(r0, TB), :] += jnp.where(p < n, prod, 0.0)
        return carry

    lax.fori_loop(0, (n + GROUP - 1) // GROUP, body, 0)


def _local_kernel(order_ref, rows_ref, cols_ref, counts_ref, table_ref, vals_ref, adj_ref, hub_ref,
                  acc_ref):
    n = acc_ref.shape[0]
    blk = 512
    for i in range(n // blk):
        sl = pl.ds(i * blk, blk)
        acc_ref[sl, :] = jnp.dot(adj_ref[sl, :], hub_ref[...], preferred_element_type=jnp.float32)
    _slot_loop(order_ref, rows_ref, cols_ref, 0, counts_ref[0], table_ref, vals_ref, acc_ref, 0)


def _remote_kernel(order_ref, rows_ref, cols_ref, counts_ref, table_ref, vals_hbm, part_ref, w_ref,
                   out_ref, acc_ref, vbuf, sems, *, lo):
    s = pl.program_id(0)

    @pl.when(s == 0)
    def _():
        start = counts_ref[0]
        n = counts_ref[1]
        groups = (n + GROUP - 1) // GROUP
        width = table_ref.shape[0] // TB

        def issue(g):
            for j in range(GROUP):
                p = g * GROUP + j
                t = order_ref[start + jnp.minimum(p, n - 1)]
                pltpu.make_async_copy(vals_hbm.at[t], vbuf.at[p], sems.at[g]).start()

        @pl.when(groups > 0)
        def _():
            issue(0)

        acc_ref[...] = jnp.zeros_like(acc_ref)

        def body(g, carry):
            @pl.when(g + 1 < groups)
            def _():
                issue(g + 1)

            base = pl.multiple_of(g * GROUP, GROUP)
            pltpu.make_async_copy(
                vals_hbm.at[pl.ds(0, GROUP)], vbuf.at[pl.ds(base, GROUP)], sems.at[g]
            ).wait()
            for j in range(GROUP):
                p = g * GROUP + j
                t = order_ref[start + jnp.minimum(p, n - 1)]
                c = jnp.clip(cols_ref[t] - lo, 0, width - 1)
                r0 = pl.multiple_of(rows_ref[t] * TB, TB)
                c0 = pl.multiple_of(c * TB, TB)
                prod = jnp.dot(vbuf[p], table_ref[pl.ds(c0, TB), :], preferred_element_type=jnp.float32)
                acc_ref[pl.ds(r0, TB), :] += jnp.where(p < n, prod, 0.0)
            return carry

        lax.fori_loop(0, groups, body, 0)

    @pl.when(s > 0)
    def _():
        blk = out_ref.shape[0]
        r0 = pl.multiple_of((s - 1) * blk, blk)
        agg = (acc_ref[pl.ds(r0, blk), :] + part_ref[...]).astype(jnp.bfloat16)
        mixed = jnp.dot(agg, w_ref[...], preferred_element_type=jnp.float32)
        out_ref[...] = jnp.maximum(mixed, 0.0).astype(out_ref.dtype)


def local_tiles(order, rows, cols, counts, table, vals, adj, hub):
    n, width = table.shape
    const2 = lambda s, *_: (0, 0)
    const3 = lambda s, *_: (0, 0, 0)
    return pl.pallas_call(
        _local_kernel,
        grid_spec=pltpu.PrefetchScalarGridSpec(
            num_scalar_prefetch=4,
            grid=(1,),
            in_specs=[
                pl.BlockSpec((n, width), const2),
                pl.BlockSpec(vals.shape, const3),
                pl.BlockSpec(adj.shape, const2),
                pl.BlockSpec(hub.shape, const2),
            ],
            out_specs=pl.BlockSpec((n, width), const2),
        ),
        out_shape=jax.ShapeDtypeStruct((n, width), jnp.float32),
    )(order, rows, cols, counts, table, vals, adj, hub)


def remote_tiles(order, rows, cols, counts, table, vals, part, weight, lo):
    n, width = part.shape
    blk = 1024
    fin_steps = n // blk
    const2 = lambda s, *_: (0, 0)
    const3 = lambda s, *_: (0, 0, 0)
    fin = lambda s, *_: (jnp.maximum(s - 1, 0), 0)
    return pl.pallas_call(
        functools.partial(_remote_kernel, lo=lo),
        grid_spec=pltpu.PrefetchScalarGridSpec(
            num_scalar_prefetch=4,
            grid=(1 + fin_steps,),
            in_specs=[
                pl.BlockSpec(table.shape, const2),
                pl.BlockSpec(memory_space=pl.ANY),
                pl.BlockSpec((blk, width), fin),
                pl.BlockSpec(weight.shape, const2),
            ],
            out_specs=pl.BlockSpec((blk, width), fin),
            scratch_shapes=[
                pltpu.VMEM((n, width), jnp.float32),
                pltpu.VMEM(vals.shape, vals.dtype),
                pltpu.SemaphoreType.DMA((vals.shape[0] // GROUP,)),
            ],
        ),
        out_shape=jax.ShapeDtypeStruct((n, width), jnp.bfloat16),
    )(order, rows, cols, counts, table, vals, part, weight)


def slot_order(cols, count, width):
    slots = cols.shape[0]
    t = jnp.arange(slots, dtype=jnp.int32)
    live = t < count
    is_a = live & (cols < width)
    is_b = live & (cols >= width)
    dead = ~live
    n_a = jnp.sum(is_a.astype(jnp.int32))
    n_b = jnp.sum(is_b.astype(jnp.int32))
    pos = jnp.where(
        is_a,
        jnp.cumsum(is_a.astype(jnp.int32)) - 1,
        jnp.where(
            is_b,
            n_a + jnp.cumsum(is_b.astype(jnp.int32)) - 1,
            n_a + n_b + jnp.cumsum(dead.astype(jnp.int32)) - 1,
        ),
    )
    order = jnp.sum(jnp.where(pos[None, :] == t[:, None], t[None, :], 0), axis=1).astype(jnp.int32)
    return order, jnp.stack([n_a, n_b]).astype(jnp.int32)


def _gather_kernel(send_ref, feat_ref, out_ref, src_ref, dst_ref):
    n = feat_ref.shape[0]
    chunk = 512
    for i in range(n // chunk):
        sl = pl.ds(i * chunk, chunk)
        src_ref[sl, :] = feat_ref[sl, :].astype(jnp.float32)

    def body(g, carry):
        base = pl.multiple_of(g * 8, 8)
        rows = [src_ref[pl.ds(send_ref[base + k], 1), :] for k in range(8)]
        dst_ref[pl.ds(base, 8), :] = jnp.concatenate(rows, axis=0)
        return carry

    lax.fori_loop(0, out_ref.shape[0] // 8, body, 0)
    for i in range(out_ref.shape[0] // chunk):
        sl = pl.ds(i * chunk, chunk)
        out_ref[sl, :] = dst_ref[sl, :].astype(out_ref.dtype)


def gather_rows(send_idx, feat):
    n, width = feat.shape
    m = send_idx.shape[0]
    return pl.pallas_call(
        _gather_kernel,
        grid_spec=pltpu.PrefetchScalarGridSpec(
            num_scalar_prefetch=1,
            grid=(1,),
            in_specs=[pl.BlockSpec((n, width), lambda s, *_: (0, 0))],
            out_specs=pl.BlockSpec((m, width), lambda s, *_: (0, 0)),
            scratch_shapes=[pltpu.VMEM((n, width), jnp.float32), pltpu.VMEM((m, width), jnp.float32)],
        ),
        out_shape=jax.ShapeDtypeStruct((m, width), feat.dtype),
    )(send_idx, feat)


def per_device(
    features,
    hub_rows,
    hub_adjacency,
    tile_row,
    tile_col,
    tile_count,
    tile_values,
    send_rows,
    weight,
):
    local = features[0, 0]
    rows = local.shape[0]
    adjacency = hub_adjacency[0, 0]
    n_blk = lax.axis_size("blk")
    hub_block = local[hub_rows[0, 0]]
    copies = jnp.broadcast_to(hub_block[None], (n_blk,) + hub_block.shape)
    hub_group = lax.all_to_all(copies, "blk", split_axis=0, concat_axis=0, tiled=True)
    hub_group = hub_group.reshape(-1, local.shape[-1])
    listing = send_rows[0, 0]
    outgoing = gather_rows(listing.reshape(-1), local)
    incoming = lax.all_to_all(outgoing, ("grp", "blk"), split_axis=0, concat_axis=0, tiled=True)
    t_rows = tile_row[0, 0]
    t_cols = tile_col[0, 0]
    vals = tile_values[0, 0]
    order, counts = slot_order(t_cols, tile_count[0, 0], rows // TB)
    part = local_tiles(order, t_rows, t_cols, counts, local, vals, adjacency, hub_group)
    out = remote_tiles(order, t_rows, t_cols, counts, incoming, vals, part, weight, rows // TB)
    return out[None, None]


def solution(mesh):
    return jax.shard_map(
        per_device,
        mesh=mesh,
        in_specs=(
            P("grp", "blk", None, None),
            P("grp", "blk", None),
            P("grp", "blk", None, None),
            P("grp", "blk", None),
            P("grp", "blk", None),
            P("grp", "blk"),
            P("grp", "blk", None, None, None),
            P("grp", "blk", None, None, None),
            P(),
        ),
        out_specs=P("grp", "blk", None, None),
        check_vma=False,
    )
```

```python
import functools

import jax
import jax.numpy as jnp
from jax import lax
from jax.experimental import pallas as pl
from jax.experimental.pallas import tpu as pltpu
from jax.sharding import PartitionSpec as P

TB = 128


GROUP = 8


def _slot_loop(order_ref, rows_ref, cols_ref, start, n, table_ref, vals_ref, acc_ref, lo):
    width = table_ref.shape[0] // TB

    def body(g, carry):
        for j in range(GROUP):
            p = g * GROUP + j
            t = order_ref[start + jnp.minimum(p, n - 1)]
            c = jnp.clip(cols_ref[t] - lo, 0, width - 1)
            r0 = pl.multiple_of(rows_ref[t] * TB, TB)
            c0 = pl.multiple_of(c * TB, TB)
            prod = jnp.dot(vals_ref[t], table_ref[pl.ds(c0, TB), :], preferred_element_type=jnp.float32)
            acc_ref[pl.ds(r0, TB), :] += jnp.where(p < n, prod, 0.0)
        return carry

    lax.fori_loop(0, (n + GROUP - 1) // GROUP, body, 0)


def _local_kernel(order_ref, rows_ref, cols_ref, counts_ref, table_ref, vals_ref, adj_ref, hub_ref,
                  acc_ref):
    n = acc_ref.shape[0]
    blk = 512
    for i in range(n // blk):
        sl = pl.ds(i * blk, blk)
        acc_ref[sl, :] = jnp.dot(adj_ref[sl, :], hub_ref[...], preferred_element_type=jnp.float32)
    _slot_loop(order_ref, rows_ref, cols_ref, 0, counts_ref[0], table_ref, vals_ref, acc_ref, 0)


def _remote_kernel(order_ref, rows_ref, cols_ref, counts_ref, table_ref, vals_hbm, acc_ref, w_ref,
                   out_ref, vbuf, sems, *, lo):
    s = pl.program_id(0)

    @pl.when(s == 0)
    def _():
        start = counts_ref[0]
        n = counts_ref[1]
        groups = (n + GROUP - 1) // GROUP
        width = table_ref.shape[0] // TB

        def issue(g):
            for j in range(GROUP):
                p = g * GROUP + j
                t = order_ref[start + jnp.minimum(p, n - 1)]
                pltpu.make_async_copy(vals_hbm.at[t], vbuf.at[p], sems.at[g]).start()

        @pl.when(groups > 0)
        def _():
            issue(0)

        def body(g, carry):
            @pl.when(g + 1 < groups)
            def _():
                issue(g + 1)

            base = pl.multiple_of(g * GROUP, GROUP)
            pltpu.make_async_copy(
                vals_hbm.at[pl.ds(0, GROUP)], vbuf.at[pl.ds(base, GROUP)], sems.at[g]
            ).wait()
            for j in range(GROUP):
                p = g * GROUP + j
                t = order_ref[start + jnp.minimum(p, n - 1)]
                c = jnp.clip(cols_ref[t] - lo, 0, width - 1)
                r0 = pl.multiple_of(rows_ref[t] * TB, TB)
                c0 = pl.multiple_of(c * TB, TB)
                prod = jnp.dot(vbuf[p], table_ref[pl.ds(c0, TB), :], preferred_element_type=jnp.float32)
                acc_ref[pl.ds(r0, TB), :] += jnp.where(p < n, prod, 0.0)
            return carry

        lax.fori_loop(0, groups, body, 0)

    @pl.when(s > 0)
    def _():
        blk = out_ref.shape[0]
        r0 = pl.multiple_of((s - 1) * blk, blk)
        agg = acc_ref[pl.ds(r0, blk), :].astype(jnp.bfloat16)
        mixed = jnp.dot(agg, w_ref[...], preferred_element_type=jnp.float32)
        out_ref[...] = jnp.maximum(mixed, 0.0).astype(out_ref.dtype)


def local_tiles(order, rows, cols, counts, table, vals, adj, hub):
    n, width = table.shape
    const2 = lambda s, *_: (0, 0)
    const3 = lambda s, *_: (0, 0, 0)
    return pl.pallas_call(
        _local_kernel,
        grid_spec=pltpu.PrefetchScalarGridSpec(
            num_scalar_prefetch=4,
            grid=(1,),
            in_specs=[
                pl.BlockSpec((n, width), const2),
                pl.BlockSpec(vals.shape, const3),
                pl.BlockSpec(adj.shape, const2),
                pl.BlockSpec(hub.shape, const2),
            ],
            out_specs=pl.BlockSpec((n, width), const2),
        ),
        out_shape=jax.ShapeDtypeStruct((n, width), jnp.float32),
    )(order, rows, cols, counts, table, vals, adj, hub)


def remote_tiles(order, rows, cols, counts, table, vals, part, weight, lo):
    n, width = part.shape
    blk = 1024
    fin_steps = n // blk
    const2 = lambda s, *_: (0, 0)
    const3 = lambda s, *_: (0, 0, 0)
    fin = lambda s, *_: (jnp.maximum(s - 1, 0), 0)
    return pl.pallas_call(
        functools.partial(_remote_kernel, lo=lo),
        grid_spec=pltpu.PrefetchScalarGridSpec(
            num_scalar_prefetch=4,
            grid=(1 + fin_steps,),
            in_specs=[
                pl.BlockSpec(table.shape, const2),
                pl.BlockSpec(memory_space=pl.ANY),
                pl.BlockSpec((n, width), const2),
                pl.BlockSpec(weight.shape, const2),
            ],
            out_specs=pl.BlockSpec((blk, width), fin),
            scratch_shapes=[
                pltpu.VMEM(vals.shape, vals.dtype),
                pltpu.SemaphoreType.DMA((vals.shape[0] // GROUP,)),
            ],
        ),
        out_shape=jax.ShapeDtypeStruct((n, width), jnp.bfloat16),
    )(order, rows, cols, counts, table, vals, part, weight)


def slot_order(cols, count, width):
    slots = cols.shape[0]
    t = jnp.arange(slots, dtype=jnp.int32)
    live = t < count
    is_a = live & (cols < width)
    is_b = live & (cols >= width)
    dead = ~live
    n_a = jnp.sum(is_a.astype(jnp.int32))
    n_b = jnp.sum(is_b.astype(jnp.int32))
    pos = jnp.where(
        is_a,
        jnp.cumsum(is_a.astype(jnp.int32)) - 1,
        jnp.where(
            is_b,
            n_a + jnp.cumsum(is_b.astype(jnp.int32)) - 1,
            n_a + n_b + jnp.cumsum(dead.astype(jnp.int32)) - 1,
        ),
    )
    order = jnp.sum(jnp.where(pos[None, :] == t[:, None], t[None, :], 0), axis=1).astype(jnp.int32)
    return order, jnp.stack([n_a, n_b]).astype(jnp.int32)


def _gather_kernel(send_ref, feat_ref, out_ref, src_ref, dst_ref):
    n = feat_ref.shape[0]
    chunk = 512
    for i in range(n // chunk):
        sl = pl.ds(i * chunk, chunk)
        src_ref[sl, :] = feat_ref[sl, :].astype(jnp.float32)

    def body(g, carry):
        base = pl.multiple_of(g * 8, 8)
        rows = [src_ref[pl.ds(send_ref[base + k], 1), :] for k in range(8)]
        dst_ref[pl.ds(base, 8), :] = jnp.concatenate(rows, axis=0)
        return carry

    lax.fori_loop(0, out_ref.shape[0] // 8, body, 0)
    for i in range(out_ref.shape[0] // chunk):
        sl = pl.ds(i * chunk, chunk)
        out_ref[sl, :] = dst_ref[sl, :].astype(out_ref.dtype)


def gather_rows(send_idx, feat):
    n, width = feat.shape
    m = send_idx.shape[0]
    return pl.pallas_call(
        _gather_kernel,
        grid_spec=pltpu.PrefetchScalarGridSpec(
            num_scalar_prefetch=1,
            grid=(1,),
            in_specs=[pl.BlockSpec((n, width), lambda s, *_: (0, 0))],
            out_specs=pl.BlockSpec((m, width), lambda s, *_: (0, 0)),
            scratch_shapes=[pltpu.VMEM((n, width), jnp.float32), pltpu.VMEM((m, width), jnp.float32)],
        ),
        out_shape=jax.ShapeDtypeStruct((m, width), feat.dtype),
    )(send_idx, feat)


def per_device(
    features,
    hub_rows,
    hub_adjacency,
    tile_row,
    tile_col,
    tile_count,
    tile_values,
    send_rows,
    weight,
):
    local = features[0, 0]
    rows = local.shape[0]
    adjacency = hub_adjacency[0, 0]
    n_blk = lax.axis_size("blk")
    hub_block = local[hub_rows[0, 0]]
    copies = jnp.broadcast_to(hub_block[None], (n_blk,) + hub_block.shape)
    hub_group = lax.all_to_all(copies, "blk", split_axis=0, concat_axis=0, tiled=True)
    hub_group = hub_group.reshape(-1, local.shape[-1])
    listing = send_rows[0, 0]
    outgoing = gather_rows(listing.reshape(-1), local)
    incoming = lax.all_to_all(outgoing, ("grp", "blk"), split_axis=0, concat_axis=0, tiled=True)
    t_rows = tile_row[0, 0]
    t_cols = tile_col[0, 0]
    vals = tile_values[0, 0]
    order, counts = slot_order(t_cols, tile_count[0, 0], rows // TB)
    part = local_tiles(order, t_rows, t_cols, counts, local, vals, adjacency, hub_group)
    out = remote_tiles(order, t_rows, t_cols, counts, incoming, vals, part, weight, rows // TB)
    return out[None, None]


def solution(mesh):
    return jax.shard_map(
        per_device,
        mesh=mesh,
        in_specs=(
            P("grp", "blk", None, None),
            P("grp", "blk", None),
            P("grp", "blk", None, None),
            P("grp", "blk", None),
            P("grp", "blk", None),
            P("grp", "blk"),
            P("grp", "blk", None, None, None),
            P("grp", "blk", None, None, None),
            P(),
        ),
        out_specs=P("grp", "blk", None, None),
        check_vma=False,
    )
```

```python
import functools

import jax
import jax.numpy as jnp
from jax import lax
from jax.experimental import pallas as pl
from jax.experimental.pallas import tpu as pltpu
from jax.sharding import PartitionSpec as P

TB = 128


GROUP = 8


def _slot_loop(order_ref, rows_ref, cols_ref, start, n, table_ref, vals_ref, acc_ref, lo):
    width = table_ref.shape[0] // TB

    def body(g, carry):
        for j in range(GROUP):
            p = g * GROUP + j
            t = order_ref[start + jnp.minimum(p, n - 1)]
            c = jnp.clip(cols_ref[t] - lo, 0, width - 1)
            r0 = pl.multiple_of(rows_ref[t] * TB, TB)
            c0 = pl.multiple_of(c * TB, TB)
            prod = jnp.dot(vals_ref[t], table_ref[pl.ds(c0, TB), :], preferred_element_type=jnp.float32)
            acc_ref[pl.ds(r0, TB), :] += jnp.where(p < n, prod, 0.0)
        return carry

    lax.fori_loop(0, (n + GROUP - 1) // GROUP, body, 0)


def _local_kernel(order_ref, rows_ref, cols_ref, counts_ref, table_ref, vals_ref, adj_ref, hub_ref,
                  acc_ref):
    n = acc_ref.shape[0]
    blk = 512
    for i in range(n // blk):
        sl = pl.ds(i * blk, blk)
        acc_ref[sl, :] = jnp.dot(adj_ref[sl, :], hub_ref[...], preferred_element_type=jnp.float32)
    _slot_loop(order_ref, rows_ref, cols_ref, 0, counts_ref[0], table_ref, vals_ref, acc_ref, 0)


def _remote_kernel(order_ref, rows_ref, cols_ref, counts_ref, pslot_ref, pvalid_ref, table_ref,
                   vals_hbm, acc_ref, w_ref, out_ref, vbuf, sems, *, lo):
    s = pl.program_id(0)

    @pl.when(s == 0)
    def _():
        npairs = counts_ref[2]
        per = GROUP // 2
        groups = (npairs + per - 1) // per
        width = table_ref.shape[0] // TB

        def issue(g):
            for j in range(GROUP):
                p = g * GROUP + j
                pltpu.make_async_copy(vals_hbm.at[pslot_ref[p]], vbuf.at[p], sems.at[g]).start()

        @pl.when(groups > 0)
        def _():
            issue(0)

        def body(g, carry):
            @pl.when(g + 1 < groups)
            def _():
                issue(g + 1)

            base = pl.multiple_of(g * GROUP, GROUP)
            pltpu.make_async_copy(
                vals_hbm.at[pl.ds(0, GROUP)], vbuf.at[pl.ds(base, GROUP)], sems.at[g]
            ).wait()
            for j in range(per):
                q = g * per + j
                pa = 2 * q
                pb = pa + 1
                ta = pslot_ref[pa]
                tb = pslot_ref[pb]
                ca = pl.multiple_of(jnp.clip(cols_ref[ta] - lo, 0, width - 1) * TB, TB)
                cb = pl.multiple_of(jnp.clip(cols_ref[tb] - lo, 0, width - 1) * TB, TB)
                r0 = pl.multiple_of(rows_ref[ta] * TB, TB)
                vb = jnp.where(pvalid_ref[pb] > 0, vbuf[pb], jnp.zeros_like(vbuf[pb]))
                lhs = jnp.concatenate([vbuf[pa], vb], axis=1)
                rhs = jnp.concatenate([table_ref[pl.ds(ca, TB), :], table_ref[pl.ds(cb, TB), :]], axis=0)
                prod = jnp.dot(lhs, rhs, preferred_element_type=jnp.float32)
                acc_ref[pl.ds(r0, TB), :] += jnp.where(q < npairs, prod, 0.0)
            return carry

        lax.fori_loop(0, groups, body, 0)

    @pl.when(s > 0)
    def _():
        blk = out_ref.shape[0]
        r0 = pl.multiple_of((s - 1) * blk, blk)
        agg = acc_ref[pl.ds(r0, blk), :].astype(jnp.bfloat16)
        mixed = jnp.dot(agg, w_ref[...], preferred_element_type=jnp.float32)
        out_ref[...] = jnp.maximum(mixed, 0.0).astype(out_ref.dtype)


def local_tiles(order, rows, cols, counts, table, vals, adj, hub):
    n, width = table.shape
    const2 = lambda s, *_: (0, 0)
    const3 = lambda s, *_: (0, 0, 0)
    return pl.pallas_call(
        _local_kernel,
        grid_spec=pltpu.PrefetchScalarGridSpec(
            num_scalar_prefetch=4,
            grid=(1,),
            in_specs=[
                pl.BlockSpec((n, width), const2),
                pl.BlockSpec(vals.shape, const3),
                pl.BlockSpec(adj.shape, const2),
                pl.BlockSpec(hub.shape, const2),
            ],
            out_specs=pl.BlockSpec((n, width), const2),
        ),
        out_shape=jax.ShapeDtypeStruct((n, width), jnp.float32),
    )(order, rows, cols, counts, table, vals, adj, hub)


def remote_tiles(order, rows, cols, counts, pslot, pvalid, table, vals, part, weight, lo):
    n, width = part.shape
    blk = 1024
    fin_steps = n // blk
    const2 = lambda s, *_: (0, 0)
    const3 = lambda s, *_: (0, 0, 0)
    fin = lambda s, *_: (jnp.maximum(s - 1, 0), 0)
    return pl.pallas_call(
        functools.partial(_remote_kernel, lo=lo),
        grid_spec=pltpu.PrefetchScalarGridSpec(
            num_scalar_prefetch=6,
            grid=(1 + fin_steps,),
            in_specs=[
                pl.BlockSpec(table.shape, const2),
                pl.BlockSpec(memory_space=pl.ANY),
                pl.BlockSpec((n, width), const2),
                pl.BlockSpec(weight.shape, const2),
            ],
            out_specs=pl.BlockSpec((blk, width), fin),
            scratch_shapes=[
                pltpu.VMEM((pslot.shape[0],) + vals.shape[1:], vals.dtype),
                pltpu.SemaphoreType.DMA((pslot.shape[0] // GROUP,)),
            ],
        ),
        out_shape=jax.ShapeDtypeStruct((n, width), jnp.bfloat16),
    )(order, rows, cols, counts, pslot, pvalid, table, vals, part, weight)


def slot_order(rows, cols, count, width, rows_total):
    slots = cols.shape[0]
    t = jnp.arange(slots, dtype=jnp.int32)
    live = t < count
    is_a = live & (cols < width)
    is_b = live & (cols >= width)
    dead = ~live
    n_a = jnp.sum(is_a.astype(jnp.int32))
    n_b = jnp.sum(is_b.astype(jnp.int32))
    pos = jnp.where(
        is_a,
        jnp.cumsum(is_a.astype(jnp.int32)) - 1,
        jnp.where(
            is_b,
            n_a + jnp.cumsum(is_b.astype(jnp.int32)) - 1,
            n_a + n_b + jnp.cumsum(dead.astype(jnp.int32)) - 1,
        ),
    )
    order = jnp.sum(jnp.where(pos[None, :] == t[:, None], t[None, :], 0), axis=1).astype(jnp.int32)
    nrow = rows_total
    rr = jnp.arange(nrow, dtype=jnp.int32)
    hit = is_b[None, :] & (rows[None, :] == rr[:, None])
    cnt = jnp.sum(hit.astype(jnp.int32), axis=1)
    pairs = (cnt + 1) // 2
    pair_off = jnp.cumsum(pairs) - pairs
    same = is_b[None, :] & (rows[None, :] == rows[:, None]) & (t[None, :] < t[:, None])
    rank = jnp.sum(same.astype(jnp.int32), axis=1)
    ppos = jnp.where(is_b, 2 * pair_off[rows] + rank, -1)
    npos = 2 * (slots + nrow) // 2
    npos = ((npos + GROUP - 1) // GROUP) * GROUP
    p = jnp.arange(npos, dtype=jnp.int32)
    at = ppos[None, :] == p[:, None]
    pvalid = jnp.any(at, axis=1)
    pslot = jnp.sum(jnp.where(at, t[None, :], 0), axis=1).astype(jnp.int32)
    partner = jnp.concatenate([pslot[:1], pslot[:-1]])
    pslot = jnp.where(pvalid, pslot, jnp.where(p % 2 == 1, partner, 0)).astype(jnp.int32)
    npairs = jnp.sum(pairs).astype(jnp.int32)
    counts = jnp.stack([n_a, n_b, npairs]).astype(jnp.int32)
    return order, counts, pslot, pvalid.astype(jnp.int32)


def _gather_kernel(send_ref, feat_ref, out_ref, src_ref, dst_ref):
    n = feat_ref.shape[0]
    chunk = 512
    for i in range(n // chunk):
        sl = pl.ds(i * chunk, chunk)
        src_ref[sl, :] = feat_ref[sl, :].astype(jnp.float32)

    def body(g, carry):
        base = pl.multiple_of(g * 8, 8)
        rows = [src_ref[pl.ds(send_ref[base + k], 1), :] for k in range(8)]
        dst_ref[pl.ds(base, 8), :] = jnp.concatenate(rows, axis=0)
        return carry

    lax.fori_loop(0, out_ref.shape[0] // 8, body, 0)
    for i in range(out_ref.shape[0] // chunk):
        sl = pl.ds(i * chunk, chunk)
        out_ref[sl, :] = dst_ref[sl, :].astype(out_ref.dtype)


def gather_rows(send_idx, feat):
    n, width = feat.shape
    m = send_idx.shape[0]
    return pl.pallas_call(
        _gather_kernel,
        grid_spec=pltpu.PrefetchScalarGridSpec(
            num_scalar_prefetch=1,
            grid=(1,),
            in_specs=[pl.BlockSpec((n, width), lambda s, *_: (0, 0))],
            out_specs=pl.BlockSpec((m, width), lambda s, *_: (0, 0)),
            scratch_shapes=[pltpu.VMEM((n, width), jnp.float32), pltpu.VMEM((m, width), jnp.float32)],
        ),
        out_shape=jax.ShapeDtypeStruct((m, width), feat.dtype),
    )(send_idx, feat)


def per_device(
    features,
    hub_rows,
    hub_adjacency,
    tile_row,
    tile_col,
    tile_count,
    tile_values,
    send_rows,
    weight,
):
    local = features[0, 0]
    rows = local.shape[0]
    adjacency = hub_adjacency[0, 0]
    n_blk = lax.axis_size("blk")
    hub_block = local[hub_rows[0, 0]]
    copies = jnp.broadcast_to(hub_block[None], (n_blk,) + hub_block.shape)
    hub_group = lax.all_to_all(copies, "blk", split_axis=0, concat_axis=0, tiled=True)
    hub_group = hub_group.reshape(-1, local.shape[-1])
    listing = send_rows[0, 0]
    outgoing = gather_rows(listing.reshape(-1), local)
    incoming = lax.all_to_all(outgoing, ("grp", "blk"), split_axis=0, concat_axis=0, tiled=True)
    t_rows = tile_row[0, 0]
    t_cols = tile_col[0, 0]
    vals = tile_values[0, 0]
    order, counts, pslot, pvalid = slot_order(t_rows, t_cols, tile_count[0, 0], rows // TB, rows // TB)
    part = local_tiles(order, t_rows, t_cols, counts, local, vals, adjacency, hub_group)
    out = remote_tiles(order, t_rows, t_cols, counts, pslot, pvalid, incoming, vals, part, weight, rows // TB)
    return out[None, None]


def solution(mesh):
    return jax.shard_map(
        per_device,
        mesh=mesh,
        in_specs=(
            P("grp", "blk", None, None),
            P("grp", "blk", None),
            P("grp", "blk", None, None),
            P("grp", "blk", None),
            P("grp", "blk", None),
            P("grp", "blk"),
            P("grp", "blk", None, None, None),
            P("grp", "blk", None, None, None),
            P(),
        ),
        out_specs=P("grp", "blk", None, None),
        check_vma=False,
    )
```

```python
import functools

import jax
import jax.numpy as jnp
from jax import lax
from jax.experimental import pallas as pl
from jax.experimental.pallas import tpu as pltpu
from jax.sharding import PartitionSpec as P

TB = 128


GROUP = 8


def _slot_loop(order_ref, rows_ref, cols_ref, start, n, table_ref, vals_ref, acc_ref, lo):
    width = table_ref.shape[0] // TB

    def body(g, carry):
        for j in range(GROUP):
            p = g * GROUP + j
            t = order_ref[start + jnp.minimum(p, n - 1)]
            c = jnp.clip(cols_ref[t] - lo, 0, width - 1)
            r0 = pl.multiple_of(rows_ref[t] * TB, TB)
            c0 = pl.multiple_of(c * TB, TB)
            prod = jnp.dot(vals_ref[t], table_ref[pl.ds(c0, TB), :], preferred_element_type=jnp.float32)
            acc_ref[pl.ds(r0, TB), :] += jnp.where(p < n, prod, 0.0)
        return carry

    lax.fori_loop(0, (n + GROUP - 1) // GROUP, body, 0)


def _local_kernel(order_ref, rows_ref, cols_ref, counts_ref, table_ref, vals_ref, adj_ref, hub_ref,
                  acc_ref):
    n = acc_ref.shape[0]
    blk = 512
    for i in range(n // blk):
        sl = pl.ds(i * blk, blk)
        acc_ref[sl, :] = jnp.dot(adj_ref[sl, :], hub_ref[...], preferred_element_type=jnp.float32)
    _slot_loop(order_ref, rows_ref, cols_ref, 0, counts_ref[0], table_ref, vals_ref, acc_ref, 0)


def _remote_kernel(order_ref, rows_ref, cols_ref, counts_ref, table_ref, vals_hbm, acc_ref, w_ref,
                   out_ref, vbuf, sems, *, lo):
    s = pl.program_id(0)

    @pl.when(s == 0)
    def _():
        start = counts_ref[0]
        n = counts_ref[1]
        groups = (n + GROUP - 1) // GROUP
        width = table_ref.shape[0] // TB

        def issue(g):
            for j in range(GROUP):
                p = g * GROUP + j
                t = order_ref[start + jnp.minimum(p, n - 1)]
                pltpu.make_async_copy(vals_hbm.at[t], vbuf.at[p], sems.at[g]).start()

        @pl.when(groups > 0)
        def _():
            issue(0)

        def body(g, carry):
            @pl.when(g + 1 < groups)
            def _():
                issue(g + 1)

            base = pl.multiple_of(g * GROUP, GROUP)
            pltpu.make_async_copy(
                vals_hbm.at[pl.ds(0, GROUP)], vbuf.at[pl.ds(base, GROUP)], sems.at[g]
            ).wait()
            for j in range(GROUP):
                p = g * GROUP + j
                t = order_ref[start + jnp.minimum(p, n - 1)]
                c = jnp.clip(cols_ref[t] - lo, 0, width - 1)
                r0 = pl.multiple_of(rows_ref[t] * TB, TB)
                c0 = pl.multiple_of(c * TB, TB)
                prod = jnp.dot(vbuf[p], table_ref[pl.ds(c0, TB), :], preferred_element_type=jnp.float32)
                acc_ref[pl.ds(r0, TB), :] += jnp.where(p < n, prod, 0.0)
            return carry

        lax.fori_loop(0, groups, body, 0)

    @pl.when(s > 0)
    def _():
        blk = out_ref.shape[0]
        r0 = pl.multiple_of((s - 1) * blk, blk)
        agg = acc_ref[pl.ds(r0, blk), :].astype(jnp.bfloat16)
        mixed = jnp.dot(agg, w_ref[...], preferred_element_type=jnp.float32)
        out_ref[...] = jnp.maximum(mixed, 0.0).astype(out_ref.dtype)


def local_tiles(order, rows, cols, counts, table, vals, adj, hub):
    n, width = table.shape
    const2 = lambda s, *_: (0, 0)
    const3 = lambda s, *_: (0, 0, 0)
    return pl.pallas_call(
        _local_kernel,
        grid_spec=pltpu.PrefetchScalarGridSpec(
            num_scalar_prefetch=4,
            grid=(1,),
            in_specs=[
                pl.BlockSpec((n, width), const2),
                pl.BlockSpec(vals.shape, const3),
                pl.BlockSpec(adj.shape, const2),
                pl.BlockSpec(hub.shape, const2),
            ],
            out_specs=pl.BlockSpec((n, width), const2),
        ),
        out_shape=jax.ShapeDtypeStruct((n, width), jnp.float32),
    )(order, rows, cols, counts, table, vals, adj, hub)


def remote_tiles(order, rows, cols, counts, table, vals, part, weight, lo):
    n, width = part.shape
    blk = 1024
    fin_steps = n // blk
    const2 = lambda s, *_: (0, 0)
    const3 = lambda s, *_: (0, 0, 0)
    fin = lambda s, *_: (jnp.maximum(s - 1, 0), 0)
    return pl.pallas_call(
        functools.partial(_remote_kernel, lo=lo),
        grid_spec=pltpu.PrefetchScalarGridSpec(
            num_scalar_prefetch=4,
            grid=(1 + fin_steps,),
            in_specs=[
                pl.BlockSpec(table.shape, const2),
                pl.BlockSpec(memory_space=pl.ANY),
                pl.BlockSpec((n, width), const2),
                pl.BlockSpec(weight.shape, const2),
            ],
            out_specs=pl.BlockSpec((blk, width), fin),
            scratch_shapes=[
                pltpu.VMEM(vals.shape, vals.dtype),
                pltpu.SemaphoreType.DMA((vals.shape[0] // GROUP,)),
            ],
        ),
        out_shape=jax.ShapeDtypeStruct((n, width), jnp.bfloat16),
    )(order, rows, cols, counts, table, vals, part, weight)


def slot_order(cols, count, width):
    slots = cols.shape[0]
    t = jnp.arange(slots, dtype=jnp.int32)
    live = t < count
    is_a = live & (cols < width)
    is_b = live & (cols >= width)
    dead = ~live
    n_a = jnp.sum(is_a.astype(jnp.int32))
    n_b = jnp.sum(is_b.astype(jnp.int32))
    pos = jnp.where(
        is_a,
        jnp.cumsum(is_a.astype(jnp.int32)) - 1,
        jnp.where(
            is_b,
            n_a + jnp.cumsum(is_b.astype(jnp.int32)) - 1,
            n_a + n_b + jnp.cumsum(dead.astype(jnp.int32)) - 1,
        ),
    )
    order = jnp.sum(jnp.where(pos[None, :] == t[:, None], t[None, :], 0), axis=1).astype(jnp.int32)
    return order, jnp.stack([n_a, n_b]).astype(jnp.int32)


def _gather_kernel(send_ref, feat_ref, out_ref, src_ref, dst_ref):
    n = feat_ref.shape[0]
    chunk = 512
    for i in range(n // chunk):
        sl = pl.ds(i * chunk, chunk)
        src_ref[sl, :] = feat_ref[sl, :].astype(jnp.float32)

    unroll = 4

    def body(g, carry):
        for u in range(unroll):
            base = pl.multiple_of((g * unroll + u) * 8, 8)
            rows = [src_ref[pl.ds(send_ref[base + k], 1), :] for k in range(8)]
            dst_ref[pl.ds(base, 8), :] = jnp.concatenate(rows, axis=0)
        return carry

    lax.fori_loop(0, out_ref.shape[0] // (8 * unroll), body, 0)
    for i in range(out_ref.shape[0] // chunk):
        sl = pl.ds(i * chunk, chunk)
        out_ref[sl, :] = dst_ref[sl, :].astype(out_ref.dtype)


def gather_rows(send_idx, feat):
    n, width = feat.shape
    m = send_idx.shape[0]
    return pl.pallas_call(
        _gather_kernel,
        grid_spec=pltpu.PrefetchScalarGridSpec(
            num_scalar_prefetch=1,
            grid=(1,),
            in_specs=[pl.BlockSpec((n, width), lambda s, *_: (0, 0))],
            out_specs=pl.BlockSpec((m, width), lambda s, *_: (0, 0)),
            scratch_shapes=[pltpu.VMEM((n, width), jnp.float32), pltpu.VMEM((m, width), jnp.float32)],
        ),
        out_shape=jax.ShapeDtypeStruct((m, width), feat.dtype),
    )(send_idx, feat)


def per_device(
    features,
    hub_rows,
    hub_adjacency,
    tile_row,
    tile_col,
    tile_count,
    tile_values,
    send_rows,
    weight,
):
    local = features[0, 0]
    rows = local.shape[0]
    adjacency = hub_adjacency[0, 0]
    n_blk = lax.axis_size("blk")
    hub_block = local[hub_rows[0, 0]]
    copies = jnp.broadcast_to(hub_block[None], (n_blk,) + hub_block.shape)
    hub_group = lax.all_to_all(copies, "blk", split_axis=0, concat_axis=0, tiled=True)
    hub_group = hub_group.reshape(-1, local.shape[-1])
    listing = send_rows[0, 0]
    outgoing = gather_rows(listing.reshape(-1), local)
    incoming = lax.all_to_all(outgoing, ("grp", "blk"), split_axis=0, concat_axis=0, tiled=True)
    t_rows = tile_row[0, 0]
    t_cols = tile_col[0, 0]
    vals = tile_values[0, 0]
    order, counts = slot_order(t_cols, tile_count[0, 0], rows // TB)
    part = local_tiles(order, t_rows, t_cols, counts, local, vals, adjacency, hub_group)
    out = remote_tiles(order, t_rows, t_cols, counts, incoming, vals, part, weight, rows // TB)
    return out[None, None]


def solution(mesh):
    return jax.shard_map(
        per_device,
        mesh=mesh,
        in_specs=(
            P("grp", "blk", None, None),
            P("grp", "blk", None),
            P("grp", "blk", None, None),
            P("grp", "blk", None),
            P("grp", "blk", None),
            P("grp", "blk"),
            P("grp", "blk", None, None, None),
            P("grp", "blk", None, None, None),
            P(),
        ),
        out_specs=P("grp", "blk", None, None),
        check_vma=False,
    )
```

```python
import functools

import jax
import jax.numpy as jnp
from jax import lax
from jax.experimental import pallas as pl
from jax.experimental.pallas import tpu as pltpu
from jax.sharding import PartitionSpec as P

TB = 128


GROUP = 8


def _slot_loop(order_ref, rows_ref, cols_ref, start, n, table_ref, vals_ref, acc_ref, lo):
    width = table_ref.shape[0] // TB

    def body(g, carry):
        for j in range(GROUP):
            p = g * GROUP + j
            t = order_ref[start + jnp.minimum(p, n - 1)]
            c = jnp.clip(cols_ref[t] - lo, 0, width - 1)
            r0 = pl.multiple_of(rows_ref[t] * TB, TB)
            c0 = pl.multiple_of(c * TB, TB)
            prod = jnp.dot(vals_ref[t], table_ref[pl.ds(c0, TB), :], preferred_element_type=jnp.float32)
            acc_ref[pl.ds(r0, TB), :] += jnp.where(p < n, prod, 0.0)
        return carry

    lax.fori_loop(0, (n + GROUP - 1) // GROUP, body, 0)


def _local_kernel(order_ref, rows_ref, cols_ref, counts_ref, table_ref, vals_ref, adj_ref, hub_ref,
                  acc_ref):
    n = acc_ref.shape[0]
    blk = 512
    for i in range(n // blk):
        sl = pl.ds(i * blk, blk)
        acc_ref[sl, :] = jnp.dot(adj_ref[sl, :], hub_ref[...], preferred_element_type=jnp.float32)
    _slot_loop(order_ref, rows_ref, cols_ref, 0, counts_ref[0], table_ref, vals_ref, acc_ref, 0)


def _remote_kernel(order_ref, rows_ref, cols_ref, counts_ref, table_ref, vals_hbm, acc_ref, w_ref,
                   out_ref, vbuf, sems, *, lo):
    s = pl.program_id(0)

    @pl.when(s == 0)
    def _():
        start = counts_ref[0]
        n = counts_ref[1]
        groups = (n + GROUP - 1) // GROUP
        width = table_ref.shape[0] // TB

        def issue(g):
            for j in range(GROUP):
                p = g * GROUP + j
                t = order_ref[start + jnp.minimum(p, n - 1)]
                pltpu.make_async_copy(vals_hbm.at[t], vbuf.at[p], sems.at[g]).start()

        @pl.when(groups > 0)
        def _():
            issue(0)

        def body(g, carry):
            @pl.when(g + 1 < groups)
            def _():
                issue(g + 1)

            base = pl.multiple_of(g * GROUP, GROUP)
            pltpu.make_async_copy(
                vals_hbm.at[pl.ds(0, GROUP)], vbuf.at[pl.ds(base, GROUP)], sems.at[g]
            ).wait()
            for j in range(GROUP):
                p = g * GROUP + j
                t = order_ref[start + jnp.minimum(p, n - 1)]
                c = jnp.clip(cols_ref[t] - lo, 0, width - 1)
                r0 = pl.multiple_of(rows_ref[t] * TB, TB)
                c0 = pl.multiple_of(c * TB, TB)
                prod = jnp.dot(vbuf[p], table_ref[pl.ds(c0, TB), :], preferred_element_type=jnp.float32)
                acc_ref[pl.ds(r0, TB), :] += jnp.where(p < n, prod, 0.0)
            return carry

        lax.fori_loop(0, groups, body, 0)

    @pl.when(s > 0)
    def _():
        blk = out_ref.shape[0]
        r0 = pl.multiple_of((s - 1) * blk, blk)
        agg = acc_ref[pl.ds(r0, blk), :].astype(jnp.bfloat16)
        mixed = jnp.dot(agg, w_ref[...], preferred_element_type=jnp.float32)
        out_ref[...] = jnp.maximum(mixed, 0.0).astype(out_ref.dtype)


def local_tiles(order, rows, cols, counts, table, vals, adj, hub):
    n, width = table.shape
    const2 = lambda s, *_: (0, 0)
    const3 = lambda s, *_: (0, 0, 0)
    return pl.pallas_call(
        _local_kernel,
        grid_spec=pltpu.PrefetchScalarGridSpec(
            num_scalar_prefetch=4,
            grid=(1,),
            in_specs=[
                pl.BlockSpec((n, width), const2),
                pl.BlockSpec(vals.shape, const3),
                pl.BlockSpec(adj.shape, const2),
                pl.BlockSpec(hub.shape, const2),
            ],
            out_specs=pl.BlockSpec((n, width), const2),
        ),
        out_shape=jax.ShapeDtypeStruct((n, width), jnp.float32),
    )(order, rows, cols, counts, table, vals, adj, hub)


def remote_tiles(order, rows, cols, counts, table, vals, part, weight, lo):
    n, width = part.shape
    blk = 1024
    fin_steps = n // blk
    const2 = lambda s, *_: (0, 0)
    const3 = lambda s, *_: (0, 0, 0)
    fin = lambda s, *_: (jnp.maximum(s - 1, 0), 0)
    return pl.pallas_call(
        functools.partial(_remote_kernel, lo=lo),
        grid_spec=pltpu.PrefetchScalarGridSpec(
            num_scalar_prefetch=4,
            grid=(1 + fin_steps,),
            in_specs=[
                pl.BlockSpec(table.shape, const2),
                pl.BlockSpec(memory_space=pl.ANY),
                pl.BlockSpec((n, width), const2),
                pl.BlockSpec(weight.shape, const2),
            ],
            out_specs=pl.BlockSpec((blk, width), fin),
            scratch_shapes=[
                pltpu.VMEM(vals.shape, vals.dtype),
                pltpu.SemaphoreType.DMA((vals.shape[0] // GROUP,)),
            ],
        ),
        out_shape=jax.ShapeDtypeStruct((n, width), jnp.bfloat16),
    )(order, rows, cols, counts, table, vals, part, weight)


def slot_order(cols, count, width):
    slots = cols.shape[0]
    t = jnp.arange(slots, dtype=jnp.int32)
    live = t < count
    is_a = live & (cols < width)
    is_b = live & (cols >= width)
    dead = ~live
    n_a = jnp.sum(is_a.astype(jnp.int32))
    n_b = jnp.sum(is_b.astype(jnp.int32))
    pos = jnp.where(
        is_a,
        jnp.cumsum(is_a.astype(jnp.int32)) - 1,
        jnp.where(
            is_b,
            n_a + jnp.cumsum(is_b.astype(jnp.int32)) - 1,
            n_a + n_b + jnp.cumsum(dead.astype(jnp.int32)) - 1,
        ),
    )
    order = jnp.sum(jnp.where(pos[None, :] == t[:, None], t[None, :], 0), axis=1).astype(jnp.int32)
    return order, jnp.stack([n_a, n_b]).astype(jnp.int32)


def _gather_kernel(send_ref, feat_ref, out_ref, src_ref, dst_ref):
    n = feat_ref.shape[0]
    chunk = 512
    for i in range(n // chunk):
        sl = pl.ds(i * chunk, chunk)
        src_ref[sl, :] = feat_ref[sl, :].astype(jnp.float32)

    per_row = send_ref.shape[1]
    unroll = per_row // 8

    def body(g, carry):
        for u in range(unroll):
            base = pl.multiple_of(g * per_row + u * 8, 8)
            rows = [src_ref[pl.ds(send_ref[g, u * 8 + k], 1), :] for k in range(8)]
            dst_ref[pl.ds(base, 8), :] = jnp.concatenate(rows, axis=0)
        return carry

    lax.fori_loop(0, send_ref.shape[0], body, 0)
    for i in range(out_ref.shape[0] // chunk):
        sl = pl.ds(i * chunk, chunk)
        out_ref[sl, :] = dst_ref[sl, :].astype(out_ref.dtype)


def gather_rows(send_idx, feat):
    n, width = feat.shape
    m = send_idx.shape[0] * send_idx.shape[1]
    return pl.pallas_call(
        _gather_kernel,
        grid_spec=pltpu.PrefetchScalarGridSpec(
            num_scalar_prefetch=1,
            grid=(1,),
            in_specs=[pl.BlockSpec((n, width), lambda s, *_: (0, 0))],
            out_specs=pl.BlockSpec((m, width), lambda s, *_: (0, 0)),
            scratch_shapes=[pltpu.VMEM((n, width), jnp.float32), pltpu.VMEM((m, width), jnp.float32)],
        ),
        out_shape=jax.ShapeDtypeStruct((m, width), feat.dtype),
    )(send_idx, feat)


def per_device(
    features,
    hub_rows,
    hub_adjacency,
    tile_row,
    tile_col,
    tile_count,
    tile_values,
    send_rows,
    weight,
):
    local = features[0, 0]
    rows = local.shape[0]
    adjacency = hub_adjacency[0, 0]
    n_blk = lax.axis_size("blk")
    hub_block = local[hub_rows[0, 0]]
    copies = jnp.broadcast_to(hub_block[None], (n_blk,) + hub_block.shape)
    hub_group = lax.all_to_all(copies, "blk", split_axis=0, concat_axis=0, tiled=True)
    hub_group = hub_group.reshape(-1, local.shape[-1])
    listing = send_rows[0, 0]
    outgoing = gather_rows(listing.reshape(-1, listing.shape[-1]), local)
    incoming = lax.all_to_all(outgoing, ("grp", "blk"), split_axis=0, concat_axis=0, tiled=True)
    t_rows = tile_row[0, 0]
    t_cols = tile_col[0, 0]
    vals = tile_values[0, 0]
    order, counts = slot_order(t_cols, tile_count[0, 0], rows // TB)
    part = local_tiles(order, t_rows, t_cols, counts, local, vals, adjacency, hub_group)
    out = remote_tiles(order, t_rows, t_cols, counts, incoming, vals, part, weight, rows // TB)
    return out[None, None]


def solution(mesh):
    return jax.shard_map(
        per_device,
        mesh=mesh,
        in_specs=(
            P("grp", "blk", None, None),
            P("grp", "blk", None),
            P("grp", "blk", None, None),
            P("grp", "blk", None),
            P("grp", "blk", None),
            P("grp", "blk"),
            P("grp", "blk", None, None, None),
            P("grp", "blk", None, None, None),
            P(),
        ),
        out_specs=P("grp", "blk", None, None),
        check_vma=False,
    )
```

```python
import functools

import jax
import jax.numpy as jnp
from jax import lax
from jax.experimental import pallas as pl
from jax.experimental.pallas import tpu as pltpu
from jax.sharding import PartitionSpec as P

TB = 128


GROUP = 8


def _slot_loop(order_ref, rows_ref, cols_ref, start, n, table_ref, vals_ref, acc_ref, lo):
    width = table_ref.shape[0] // TB

    def body(g, carry):
        for j in range(GROUP):
            p = g * GROUP + j
            t = order_ref[start + jnp.minimum(p, n - 1)]
            c = jnp.clip(cols_ref[t] - lo, 0, width - 1)
            r0 = pl.multiple_of(rows_ref[t] * TB, TB)
            c0 = pl.multiple_of(c * TB, TB)
            prod = jnp.dot(vals_ref[t], table_ref[pl.ds(c0, TB), :], preferred_element_type=jnp.float32)
            acc_ref[pl.ds(r0, TB), :] += jnp.where(p < n, prod, 0.0)
        return carry

    lax.fori_loop(0, (n + GROUP - 1) // GROUP, body, 0)


def _local_kernel(order_ref, rows_ref, cols_ref, counts_ref, table_ref, vals_ref, adj_ref, hub_ref,
                  acc_ref):
    n = acc_ref.shape[0]
    blk = 512
    for i in range(n // blk):
        sl = pl.ds(i * blk, blk)
        acc_ref[sl, :] = jnp.dot(adj_ref[sl, :], hub_ref[...], preferred_element_type=jnp.float32)
    _slot_loop(order_ref, rows_ref, cols_ref, 0, counts_ref[0], table_ref, vals_ref, acc_ref, 0)


def _remote_kernel(order_ref, rows_ref, cols_ref, counts_ref, table_ref, vals_hbm, acc_ref, w_ref,
                   out_ref, vbuf, sems, *, lo):
    s = pl.program_id(0)

    @pl.when(s == 0)
    def _():
        start = counts_ref[0]
        n = counts_ref[1]
        groups = (n + GROUP - 1) // GROUP
        width = table_ref.shape[0] // TB

        def issue(g):
            for j in range(GROUP):
                p = g * GROUP + j
                t = order_ref[start + jnp.minimum(p, n - 1)]
                pltpu.make_async_copy(vals_hbm.at[t], vbuf.at[p], sems.at[g]).start()

        @pl.when(groups > 0)
        def _():
            issue(0)

        def body(g, carry):
            @pl.when(g + 1 < groups)
            def _():
                issue(g + 1)

            base = pl.multiple_of(g * GROUP, GROUP)
            pltpu.make_async_copy(
                vals_hbm.at[pl.ds(0, GROUP)], vbuf.at[pl.ds(base, GROUP)], sems.at[g]
            ).wait()
            for j in range(GROUP):
                p = g * GROUP + j
                t = order_ref[start + jnp.minimum(p, n - 1)]
                c = jnp.clip(cols_ref[t] - lo, 0, width - 1)
                r0 = pl.multiple_of(rows_ref[t] * TB, TB)
                c0 = pl.multiple_of(c * TB, TB)
                prod = jnp.dot(vbuf[p], table_ref[pl.ds(c0, TB), :], preferred_element_type=jnp.float32)
                acc_ref[pl.ds(r0, TB), :] += jnp.where(p < n, prod, 0.0)
            return carry

        lax.fori_loop(0, groups, body, 0)

    @pl.when(s > 0)
    def _():
        blk = out_ref.shape[0]
        r0 = pl.multiple_of((s - 1) * blk, blk)
        agg = acc_ref[pl.ds(r0, blk), :].astype(jnp.bfloat16)
        mixed = jnp.dot(agg, w_ref[...], preferred_element_type=jnp.float32)
        out_ref[...] = jnp.maximum(mixed, 0.0).astype(out_ref.dtype)


def local_tiles(order, rows, cols, counts, table, vals, adj, hub):
    n, width = table.shape
    const2 = lambda s, *_: (0, 0)
    const3 = lambda s, *_: (0, 0, 0)
    return pl.pallas_call(
        _local_kernel,
        grid_spec=pltpu.PrefetchScalarGridSpec(
            num_scalar_prefetch=4,
            grid=(1,),
            in_specs=[
                pl.BlockSpec((n, width), const2),
                pl.BlockSpec(vals.shape, const3),
                pl.BlockSpec(adj.shape, const2),
                pl.BlockSpec(hub.shape, const2),
            ],
            out_specs=pl.BlockSpec((n, width), const2),
        ),
        out_shape=jax.ShapeDtypeStruct((n, width), jnp.float32),
    )(order, rows, cols, counts, table, vals, adj, hub)


def remote_tiles(order, rows, cols, counts, table, vals, part, weight, lo):
    n, width = part.shape
    blk = 1024
    fin_steps = n // blk
    const2 = lambda s, *_: (0, 0)
    const3 = lambda s, *_: (0, 0, 0)
    fin = lambda s, *_: (jnp.maximum(s - 1, 0), 0)
    return pl.pallas_call(
        functools.partial(_remote_kernel, lo=lo),
        grid_spec=pltpu.PrefetchScalarGridSpec(
            num_scalar_prefetch=4,
            grid=(1 + fin_steps,),
            in_specs=[
                pl.BlockSpec(table.shape, const2),
                pl.BlockSpec(memory_space=pl.ANY),
                pl.BlockSpec((n, width), const2),
                pl.BlockSpec(weight.shape, const2),
            ],
            out_specs=pl.BlockSpec((blk, width), fin),
            scratch_shapes=[
                pltpu.VMEM(vals.shape, vals.dtype),
                pltpu.SemaphoreType.DMA((vals.shape[0] // GROUP,)),
            ],
        ),
        out_shape=jax.ShapeDtypeStruct((n, width), jnp.bfloat16),
    )(order, rows, cols, counts, table, vals, part, weight)


def slot_order(cols, count, width):
    slots = cols.shape[0]
    t = jnp.arange(slots, dtype=jnp.int32)
    live = t < count
    is_a = live & (cols < width)
    is_b = live & (cols >= width)
    dead = ~live
    n_a = jnp.sum(is_a.astype(jnp.int32))
    n_b = jnp.sum(is_b.astype(jnp.int32))
    pos = jnp.where(
        is_a,
        jnp.cumsum(is_a.astype(jnp.int32)) - 1,
        jnp.where(
            is_b,
            n_a + jnp.cumsum(is_b.astype(jnp.int32)) - 1,
            n_a + n_b + jnp.cumsum(dead.astype(jnp.int32)) - 1,
        ),
    )
    order = jnp.sum(jnp.where(pos[None, :] == t[:, None], t[None, :], 0), axis=1).astype(jnp.int32)
    return order, jnp.stack([n_a, n_b]).astype(jnp.int32)


def _gather_kernel(send_ref, feat_ref, out_ref, src_ref, dst_ref):
    n = feat_ref.shape[0]
    chunk = 512
    for i in range(n // chunk):
        sl = pl.ds(i * chunk, chunk)
        src_ref[sl, :] = feat_ref[sl, :].astype(jnp.float32)

    per_row = send_ref.shape[1]
    unroll = per_row // 8

    def body(g, carry):
        for u in range(unroll):
            base = pl.multiple_of(g * per_row + u * 8, 8)
            rows = [src_ref[pl.ds(send_ref[g, u * 8 + k], 1), :] for k in range(8)]
            dst_ref[pl.ds(base, 8), :] = jnp.concatenate(rows, axis=0)
        return carry

    lax.fori_loop(0, send_ref.shape[0], body, 0)
    for i in range(out_ref.shape[0] // chunk):
        sl = pl.ds(i * chunk, chunk)
        out_ref[sl, :] = dst_ref[sl, :].astype(out_ref.dtype)


def gather_rows(send_idx, feat):
    n, width = feat.shape
    m = send_idx.shape[0] * send_idx.shape[1]
    return pl.pallas_call(
        _gather_kernel,
        grid_spec=pltpu.PrefetchScalarGridSpec(
            num_scalar_prefetch=1,
            grid=(1,),
            in_specs=[pl.BlockSpec((n, width), lambda s, *_: (0, 0))],
            out_specs=pl.BlockSpec((m, width), lambda s, *_: (0, 0)),
            scratch_shapes=[pltpu.VMEM((n, width), jnp.float32), pltpu.VMEM((m, width), jnp.float32)],
        ),
        out_shape=jax.ShapeDtypeStruct((m, width), feat.dtype),
    )(send_idx, feat)


def per_device(
    features,
    hub_rows,
    hub_adjacency,
    tile_row,
    tile_col,
    tile_count,
    tile_values,
    send_rows,
    weight,
):
    local = features[0, 0]
    rows = local.shape[0]
    adjacency = hub_adjacency[0, 0]
    n_blk = lax.axis_size("blk")
    picks = hub_rows[0, 0][:, None] == jnp.arange(rows, dtype=jnp.int32)[None, :]
    hub_block = jnp.dot(
        picks.astype(local.dtype), local, preferred_element_type=jnp.float32
    ).astype(local.dtype)
    copies = jnp.broadcast_to(hub_block[None], (n_blk,) + hub_block.shape)
    hub_group = lax.all_to_all(copies, "blk", split_axis=0, concat_axis=0, tiled=True)
    hub_group = hub_group.reshape(-1, local.shape[-1])
    listing = send_rows[0, 0]
    outgoing = gather_rows(listing.reshape(-1, listing.shape[-1]), local)
    incoming = lax.all_to_all(outgoing, ("grp", "blk"), split_axis=0, concat_axis=0, tiled=True)
    t_rows = tile_row[0, 0]
    t_cols = tile_col[0, 0]
    vals = tile_values[0, 0]
    order, counts = slot_order(t_cols, tile_count[0, 0], rows // TB)
    part = local_tiles(order, t_rows, t_cols, counts, local, vals, adjacency, hub_group)
    out = remote_tiles(order, t_rows, t_cols, counts, incoming, vals, part, weight, rows // TB)
    return out[None, None]


def solution(mesh):
    return jax.shard_map(
        per_device,
        mesh=mesh,
        in_specs=(
            P("grp", "blk", None, None),
            P("grp", "blk", None),
            P("grp", "blk", None, None),
            P("grp", "blk", None),
            P("grp", "blk", None),
            P("grp", "blk"),
            P("grp", "blk", None, None, None),
            P("grp", "blk", None, None, None),
            P(),
        ),
        out_specs=P("grp", "blk", None, None),
        check_vma=False,
    )
```

```python
import functools

import jax
import jax.numpy as jnp
from jax import lax
from jax.experimental import pallas as pl
from jax.experimental.pallas import tpu as pltpu
from jax.sharding import PartitionSpec as P

TB = 128


GROUP = 8


def _slot_loop(order_ref, rows_ref, cols_ref, start, n, table_ref, vals_ref, acc_ref, lo):
    width = table_ref.shape[0] // TB

    def body(g, carry):
        for j in range(GROUP):
            p = g * GROUP + j
            t = order_ref[start + jnp.minimum(p, n - 1)]
            c = jnp.clip(cols_ref[t] - lo, 0, width - 1)
            r0 = pl.multiple_of(rows_ref[t] * TB, TB)
            c0 = pl.multiple_of(c * TB, TB)
            prod = jnp.dot(vals_ref[t], table_ref[pl.ds(c0, TB), :], preferred_element_type=jnp.float32)
            acc_ref[pl.ds(r0, TB), :] += jnp.where(p < n, prod, 0.0)
        return carry

    lax.fori_loop(0, (n + GROUP - 1) // GROUP, body, 0)


def _local_kernel(order_ref, rows_ref, cols_ref, counts_ref, table_ref, vals_ref, adj_ref, hub_ref,
                  acc_ref):
    n = acc_ref.shape[0]
    blk = 512
    for i in range(n // blk):
        sl = pl.ds(i * blk, blk)
        acc_ref[sl, :] = jnp.dot(adj_ref[sl, :], hub_ref[...], preferred_element_type=jnp.float32)
    _slot_loop(order_ref, rows_ref, cols_ref, 0, counts_ref[0], table_ref, vals_ref, acc_ref, 0)


def _remote_kernel(order_ref, rows_ref, cols_ref, counts_ref, table_ref, vals_hbm, acc_ref, w_ref,
                   out_ref, vbuf, sems, *, lo):
    s = pl.program_id(0)

    @pl.when(s == 0)
    def _():
        start = counts_ref[0]
        n = counts_ref[1]
        groups = (n + GROUP - 1) // GROUP
        width = table_ref.shape[0] // TB

        def issue(g):
            for j in range(GROUP):
                p = g * GROUP + j
                t = order_ref[start + jnp.minimum(p, n - 1)]
                pltpu.make_async_copy(vals_hbm.at[t], vbuf.at[p], sems.at[g]).start()

        @pl.when(groups > 0)
        def _():
            issue(0)

        def body(g, carry):
            @pl.when(g + 1 < groups)
            def _():
                issue(g + 1)

            base = pl.multiple_of(g * GROUP, GROUP)
            pltpu.make_async_copy(
                vals_hbm.at[pl.ds(0, GROUP)], vbuf.at[pl.ds(base, GROUP)], sems.at[g]
            ).wait()
            for j in range(GROUP):
                p = g * GROUP + j
                t = order_ref[start + jnp.minimum(p, n - 1)]
                c = jnp.clip(cols_ref[t] - lo, 0, width - 1)
                r0 = pl.multiple_of(rows_ref[t] * TB, TB)
                c0 = pl.multiple_of(c * TB, TB)
                prod = jnp.dot(vbuf[p], table_ref[pl.ds(c0, TB), :], preferred_element_type=jnp.float32)
                acc_ref[pl.ds(r0, TB), :] += jnp.where(p < n, prod, 0.0)
            return carry

        lax.fori_loop(0, groups, body, 0)

    @pl.when(s > 0)
    def _():
        blk = out_ref.shape[0]
        r0 = pl.multiple_of((s - 1) * blk, blk)
        agg = acc_ref[pl.ds(r0, blk), :].astype(jnp.bfloat16)
        mixed = jnp.dot(agg, w_ref[...], preferred_element_type=jnp.float32)
        out_ref[...] = jnp.maximum(mixed, 0.0).astype(out_ref.dtype)


def local_tiles(order, rows, cols, counts, table, vals, adj, hub):
    n, width = table.shape
    const2 = lambda s, *_: (0, 0)
    const3 = lambda s, *_: (0, 0, 0)
    return pl.pallas_call(
        _local_kernel,
        grid_spec=pltpu.PrefetchScalarGridSpec(
            num_scalar_prefetch=4,
            grid=(1,),
            in_specs=[
                pl.BlockSpec((n, width), const2),
                pl.BlockSpec(vals.shape, const3),
                pl.BlockSpec(adj.shape, const2),
                pl.BlockSpec(hub.shape, const2),
            ],
            out_specs=pl.BlockSpec((n, width), const2),
        ),
        out_shape=jax.ShapeDtypeStruct((n, width), jnp.float32),
    )(order, rows, cols, counts, table, vals, adj, hub)


def remote_tiles(order, rows, cols, counts, table, vals, part, weight, lo):
    n, width = part.shape
    blk = 1024
    fin_steps = n // blk
    const2 = lambda s, *_: (0, 0)
    const3 = lambda s, *_: (0, 0, 0)
    fin = lambda s, *_: (jnp.maximum(s - 1, 0), 0)
    return pl.pallas_call(
        functools.partial(_remote_kernel, lo=lo),
        grid_spec=pltpu.PrefetchScalarGridSpec(
            num_scalar_prefetch=4,
            grid=(1 + fin_steps,),
            in_specs=[
                pl.BlockSpec(table.shape, const2),
                pl.BlockSpec(memory_space=pl.ANY),
                pl.BlockSpec((n, width), const2),
                pl.BlockSpec(weight.shape, const2),
            ],
            out_specs=pl.BlockSpec((blk, width), fin),
            scratch_shapes=[
                pltpu.VMEM(vals.shape, vals.dtype),
                pltpu.SemaphoreType.DMA((vals.shape[0] // GROUP,)),
            ],
        ),
        out_shape=jax.ShapeDtypeStruct((n, width), jnp.bfloat16),
    )(order, rows, cols, counts, table, vals, part, weight)


def slot_order(cols, count, width):
    slots = cols.shape[0]
    t = jnp.arange(slots, dtype=jnp.int32)
    live = t < count
    is_a = live & (cols < width)
    is_b = live & (cols >= width)
    dead = ~live
    n_a = jnp.sum(is_a.astype(jnp.int32))
    n_b = jnp.sum(is_b.astype(jnp.int32))
    pos = jnp.where(
        is_a,
        jnp.cumsum(is_a.astype(jnp.int32)) - 1,
        jnp.where(
            is_b,
            n_a + jnp.cumsum(is_b.astype(jnp.int32)) - 1,
            n_a + n_b + jnp.cumsum(dead.astype(jnp.int32)) - 1,
        ),
    )
    order = jnp.sum(jnp.where(pos[None, :] == t[:, None], t[None, :], 0), axis=1).astype(jnp.int32)
    return order, jnp.stack([n_a, n_b]).astype(jnp.int32)


def _gather_kernel(send_ref, feat_ref, out_ref, src_ref):
    n = feat_ref.shape[0]
    chunk = 512
    for i in range(n // chunk):
        sl = pl.ds(i * chunk, chunk)
        src_ref[sl, :] = feat_ref[sl, :].astype(jnp.float32)

    per_row = send_ref.shape[1]

    def body(g, carry):
        for h in range(per_row // 16):
            base = pl.multiple_of(g * per_row + h * 16, 16)
            rows = [src_ref[pl.ds(send_ref[g, h * 16 + k], 1), :] for k in range(16)]
            out_ref[pl.ds(base, 16), :] = jnp.concatenate(rows, axis=0).astype(out_ref.dtype)
        return carry

    lax.fori_loop(0, send_ref.shape[0], body, 0)


def gather_rows(send_idx, feat):
    n, width = feat.shape
    m = send_idx.shape[0] * send_idx.shape[1]
    return pl.pallas_call(
        _gather_kernel,
        grid_spec=pltpu.PrefetchScalarGridSpec(
            num_scalar_prefetch=1,
            grid=(1,),
            in_specs=[pl.BlockSpec((n, width), lambda s, *_: (0, 0))],
            out_specs=pl.BlockSpec((m, width), lambda s, *_: (0, 0)),
            scratch_shapes=[pltpu.VMEM((n, width), jnp.float32)],
        ),
        out_shape=jax.ShapeDtypeStruct((m, width), feat.dtype),
    )(send_idx, feat)


def per_device(
    features,
    hub_rows,
    hub_adjacency,
    tile_row,
    tile_col,
    tile_count,
    tile_values,
    send_rows,
    weight,
):
    local = features[0, 0]
    rows = local.shape[0]
    adjacency = hub_adjacency[0, 0]
    n_blk = lax.axis_size("blk")
    picks = hub_rows[0, 0][:, None] == jnp.arange(rows, dtype=jnp.int32)[None, :]
    hub_block = jnp.dot(
        picks.astype(local.dtype), local, preferred_element_type=jnp.float32
    ).astype(local.dtype)
    copies = jnp.broadcast_to(hub_block[None], (n_blk,) + hub_block.shape)
    hub_group = lax.all_to_all(copies, "blk", split_axis=0, concat_axis=0, tiled=True)
    hub_group = hub_group.reshape(-1, local.shape[-1])
    listing = send_rows[0, 0]
    outgoing = gather_rows(listing.reshape(-1, listing.shape[-1]), local)
    incoming = lax.all_to_all(outgoing, ("grp", "blk"), split_axis=0, concat_axis=0, tiled=True)
    t_rows = tile_row[0, 0]
    t_cols = tile_col[0, 0]
    vals = tile_values[0, 0]
    order, counts = slot_order(t_cols, tile_count[0, 0], rows // TB)
    part = local_tiles(order, t_rows, t_cols, counts, local, vals, adjacency, hub_group)
    out = remote_tiles(order, t_rows, t_cols, counts, incoming, vals, part, weight, rows // TB)
    return out[None, None]


def solution(mesh):
    return jax.shard_map(
        per_device,
        mesh=mesh,
        in_specs=(
            P("grp", "blk", None, None),
            P("grp", "blk", None),
            P("grp", "blk", None, None),
            P("grp", "blk", None),
            P("grp", "blk", None),
            P("grp", "blk"),
            P("grp", "blk", None, None, None),
            P("grp", "blk", None, None, None),
            P(),
        ),
        out_specs=P("grp", "blk", None, None),
        check_vma=False,
    )
```

```python
import functools

import jax
import jax.numpy as jnp
from jax import lax
from jax.experimental import pallas as pl
from jax.experimental.pallas import tpu as pltpu
from jax.sharding import PartitionSpec as P

TB = 128


GROUP = 8


def _slot_loop(order_ref, rows_ref, cols_ref, start, n, table_ref, vals_ref, acc_ref, lo):
    width = table_ref.shape[0] // TB

    def body(g, carry):
        for j in range(GROUP):
            p = g * GROUP + j
            t = order_ref[start + jnp.minimum(p, n - 1)]
            c = jnp.clip(cols_ref[t] - lo, 0, width - 1)
            r0 = pl.multiple_of(rows_ref[t] * TB, TB)
            c0 = pl.multiple_of(c * TB, TB)
            prod = jnp.dot(vals_ref[t], table_ref[pl.ds(c0, TB), :], preferred_element_type=jnp.float32)
            acc_ref[pl.ds(r0, TB), :] += jnp.where(p < n, prod, 0.0)
        return carry

    lax.fori_loop(0, (n + GROUP - 1) // GROUP, body, 0)


def _local_kernel(order_ref, rows_ref, cols_ref, counts_ref, table_ref, vals_ref, adj_ref, hub_ref,
                  acc_ref):
    n = acc_ref.shape[0]
    blk = 512
    for i in range(n // blk):
        sl = pl.ds(i * blk, blk)
        acc_ref[sl, :] = jnp.dot(adj_ref[sl, :], hub_ref[...], preferred_element_type=jnp.float32)
    _slot_loop(order_ref, rows_ref, cols_ref, 0, counts_ref[0], table_ref, vals_ref, acc_ref, 0)


def _remote_kernel(order_ref, rows_ref, cols_ref, counts_ref, table_ref, vals_hbm, acc_ref, w_ref,
                   out_ref, vbuf, sems, *, lo):
    s = pl.program_id(0)

    @pl.when(s == 0)
    def _():
        start = counts_ref[0]
        n = counts_ref[1]
        groups = (n + GROUP - 1) // GROUP
        width = table_ref.shape[0] // TB

        def issue(g):
            for j in range(GROUP):
                p = g * GROUP + j
                t = order_ref[start + jnp.minimum(p, n - 1)]
                pltpu.make_async_copy(vals_hbm.at[t], vbuf.at[p], sems.at[g]).start()

        @pl.when(groups > 0)
        def _():
            issue(0)

        def body(g, carry):
            @pl.when(g + 1 < groups)
            def _():
                issue(g + 1)

            base = pl.multiple_of(g * GROUP, GROUP)
            pltpu.make_async_copy(
                vals_hbm.at[pl.ds(0, GROUP)], vbuf.at[pl.ds(base, GROUP)], sems.at[g]
            ).wait()
            for j in range(GROUP):
                p = g * GROUP + j
                t = order_ref[start + jnp.minimum(p, n - 1)]
                c = jnp.clip(cols_ref[t] - lo, 0, width - 1)
                r0 = pl.multiple_of(rows_ref[t] * TB, TB)
                c0 = pl.multiple_of(c * TB, TB)
                prod = jnp.dot(vbuf[p], table_ref[pl.ds(c0, TB), :], preferred_element_type=jnp.float32)
                acc_ref[pl.ds(r0, TB), :] += jnp.where(p < n, prod, 0.0)
            return carry

        lax.fori_loop(0, groups, body, 0)

    @pl.when(s > 0)
    def _():
        blk = out_ref.shape[0]
        r0 = pl.multiple_of((s - 1) * blk, blk)
        agg = acc_ref[pl.ds(r0, blk), :].astype(jnp.bfloat16)
        mixed = jnp.dot(agg, w_ref[...], preferred_element_type=jnp.float32)
        out_ref[...] = jnp.maximum(mixed, 0.0).astype(out_ref.dtype)


def local_tiles(order, rows, cols, counts, table, vals, adj, hub):
    n, width = table.shape
    const2 = lambda s, *_: (0, 0)
    const3 = lambda s, *_: (0, 0, 0)
    return pl.pallas_call(
        _local_kernel,
        grid_spec=pltpu.PrefetchScalarGridSpec(
            num_scalar_prefetch=4,
            grid=(1,),
            in_specs=[
                pl.BlockSpec((n, width), const2),
                pl.BlockSpec(vals.shape, const3),
                pl.BlockSpec(adj.shape, const2),
                pl.BlockSpec(hub.shape, const2),
            ],
            out_specs=pl.BlockSpec((n, width), const2),
        ),
        out_shape=jax.ShapeDtypeStruct((n, width), jnp.float32),
    )(order, rows, cols, counts, table, vals, adj, hub)


def remote_tiles(order, rows, cols, counts, table, vals, part, weight, lo):
    n, width = part.shape
    blk = 1024
    fin_steps = n // blk
    const2 = lambda s, *_: (0, 0)
    const3 = lambda s, *_: (0, 0, 0)
    fin = lambda s, *_: (jnp.maximum(s - 1, 0), 0)
    return pl.pallas_call(
        functools.partial(_remote_kernel, lo=lo),
        grid_spec=pltpu.PrefetchScalarGridSpec(
            num_scalar_prefetch=4,
            grid=(1 + fin_steps,),
            in_specs=[
                pl.BlockSpec(table.shape, const2),
                pl.BlockSpec(memory_space=pl.ANY),
                pl.BlockSpec((n, width), const2),
                pl.BlockSpec(weight.shape, const2),
            ],
            out_specs=pl.BlockSpec((blk, width), fin),
            scratch_shapes=[
                pltpu.VMEM(vals.shape, vals.dtype),
                pltpu.SemaphoreType.DMA((vals.shape[0] // GROUP,)),
            ],
        ),
        out_shape=jax.ShapeDtypeStruct((n, width), jnp.bfloat16),
    )(order, rows, cols, counts, table, vals, part, weight)


def slot_order(cols, count, width):
    slots = cols.shape[0]
    t = jnp.arange(slots, dtype=jnp.int32)
    live = t < count
    is_a = live & (cols < width)
    is_b = live & (cols >= width)
    dead = ~live
    n_a = jnp.sum(is_a.astype(jnp.int32))
    n_b = jnp.sum(is_b.astype(jnp.int32))
    pos = jnp.where(
        is_a,
        jnp.cumsum(is_a.astype(jnp.int32)) - 1,
        jnp.where(
            is_b,
            n_a + jnp.cumsum(is_b.astype(jnp.int32)) - 1,
            n_a + n_b + jnp.cumsum(dead.astype(jnp.int32)) - 1,
        ),
    )
    order = jnp.sum(jnp.where(pos[None, :] == t[:, None], t[None, :], 0), axis=1).astype(jnp.int32)
    return order, jnp.stack([n_a, n_b]).astype(jnp.int32)


def _gather_kernel(send_ref, feat_ref, out_ref, src_ref):
    n = feat_ref.shape[0]
    chunk = 512
    for i in range(n // chunk):
        sl = pl.ds(i * chunk, chunk)
        src_ref[sl, :] = feat_ref[sl, :].astype(jnp.float32)

    per_row = send_ref.shape[1]

    def body(g, carry):
        for h in range(per_row // 16):
            base = pl.multiple_of(g * per_row + h * 16, 16)
            rows = [src_ref[pl.ds(send_ref[g, h * 16 + k], 1), :] for k in range(16)]
            out_ref[pl.ds(base, 16), :] = jnp.concatenate(rows, axis=0).astype(out_ref.dtype)
        return carry

    lax.fori_loop(0, send_ref.shape[0], body, 0)


def gather_rows(send_idx, feat):
    n, width = feat.shape
    m = send_idx.shape[0] * send_idx.shape[1]
    return pl.pallas_call(
        _gather_kernel,
        grid_spec=pltpu.PrefetchScalarGridSpec(
            num_scalar_prefetch=1,
            grid=(1,),
            in_specs=[pl.BlockSpec((n, width), lambda s, *_: (0, 0))],
            out_specs=pl.BlockSpec((m, width), lambda s, *_: (0, 0)),
            scratch_shapes=[pltpu.VMEM((n, width), jnp.float32)],
        ),
        out_shape=jax.ShapeDtypeStruct((m, width), feat.dtype),
    )(send_idx, feat)


def per_device(
    features,
    hub_rows,
    hub_adjacency,
    tile_row,
    tile_col,
    tile_count,
    tile_values,
    send_rows,
    weight,
):
    local = features[0, 0]
    rows = local.shape[0]
    adjacency = hub_adjacency[0, 0]
    n_blk = lax.axis_size("blk")
    hub_idx = jnp.tile(hub_rows[0, 0], n_blk)
    picks = hub_idx[:, None] == jnp.arange(rows, dtype=jnp.int32)[None, :]
    copies = jnp.dot(
        picks.astype(local.dtype), local, preferred_element_type=jnp.float32
    ).astype(local.dtype).reshape(n_blk, -1, local.shape[-1])
    hub_group = lax.all_to_all(copies, "blk", split_axis=0, concat_axis=0, tiled=True)
    hub_group = hub_group.reshape(-1, local.shape[-1])
    listing = send_rows[0, 0]
    outgoing = gather_rows(listing.reshape(-1, listing.shape[-1]), local)
    incoming = lax.all_to_all(outgoing, ("grp", "blk"), split_axis=0, concat_axis=0, tiled=True)
    t_rows = tile_row[0, 0]
    t_cols = tile_col[0, 0]
    vals = tile_values[0, 0]
    order, counts = slot_order(t_cols, tile_count[0, 0], rows // TB)
    part = local_tiles(order, t_rows, t_cols, counts, local, vals, adjacency, hub_group)
    out = remote_tiles(order, t_rows, t_cols, counts, incoming, vals, part, weight, rows // TB)
    return out[None, None]


def solution(mesh):
    return jax.shard_map(
        per_device,
        mesh=mesh,
        in_specs=(
            P("grp", "blk", None, None),
            P("grp", "blk", None),
            P("grp", "blk", None, None),
            P("grp", "blk", None),
            P("grp", "blk", None),
            P("grp", "blk"),
            P("grp", "blk", None, None, None),
            P("grp", "blk", None, None, None),
            P(),
        ),
        out_specs=P("grp", "blk", None, None),
        check_vma=False,
    )
```

```python
import functools

import jax
import jax.numpy as jnp
from jax import lax
from jax.experimental import pallas as pl
from jax.experimental.pallas import tpu as pltpu
from jax.sharding import PartitionSpec as P

TB = 128


GROUP = 8


def _slot_loop(order_ref, rows_ref, cols_ref, start, n, table_ref, vals_ref, acc_ref, lo):
    width = table_ref.shape[0] // TB

    def body(g, carry):
        for j in range(GROUP):
            p = g * GROUP + j
            t = order_ref[start + jnp.minimum(p, n - 1)]
            c = jnp.clip(cols_ref[t] - lo, 0, width - 1)
            r0 = pl.multiple_of(rows_ref[t] * TB, TB)
            c0 = pl.multiple_of(c * TB, TB)
            prod = jnp.dot(vals_ref[t], table_ref[pl.ds(c0, TB), :], preferred_element_type=jnp.float32)
            acc_ref[pl.ds(r0, TB), :] += jnp.where(p < n, prod, 0.0)
        return carry

    lax.fori_loop(0, (n + GROUP - 1) // GROUP, body, 0)


def _local_kernel(order_ref, rows_ref, cols_ref, counts_ref, table_ref, vals_ref, adj_ref, hub_ref,
                  acc_ref):
    n = acc_ref.shape[0]
    blk = 512
    for i in range(n // blk):
        sl = pl.ds(i * blk, blk)
        acc_ref[sl, :] = jnp.dot(adj_ref[sl, :], hub_ref[...], preferred_element_type=jnp.float32)
    _slot_loop(order_ref, rows_ref, cols_ref, 0, counts_ref[0], table_ref, vals_ref, acc_ref, 0)


def _remote_kernel(order_ref, rows_ref, cols_ref, counts_ref, table_ref, vals_hbm, acc_ref, w_ref,
                   out_ref, vbuf, sems, *, lo):
    s = pl.program_id(0)

    @pl.when(s == 0)
    def _():
        start = counts_ref[0]
        n = counts_ref[1]
        groups = (n + GROUP - 1) // GROUP
        width = table_ref.shape[0] // TB

        def issue(g):
            for j in range(GROUP):
                p = g * GROUP + j
                t = order_ref[start + jnp.minimum(p, n - 1)]
                pltpu.make_async_copy(vals_hbm.at[t], vbuf.at[p], sems.at[g]).start()

        @pl.when(groups > 0)
        def _():
            issue(0)

        def body(g, carry):
            @pl.when(g + 1 < groups)
            def _():
                issue(g + 1)

            base = pl.multiple_of(g * GROUP, GROUP)
            pltpu.make_async_copy(
                vals_hbm.at[pl.ds(0, GROUP)], vbuf.at[pl.ds(base, GROUP)], sems.at[g]
            ).wait()
            for j in range(GROUP):
                p = g * GROUP + j
                t = order_ref[start + jnp.minimum(p, n - 1)]
                c = jnp.clip(cols_ref[t] - lo, 0, width - 1)
                r0 = pl.multiple_of(rows_ref[t] * TB, TB)
                c0 = pl.multiple_of(c * TB, TB)
                prod = jnp.dot(vbuf[p], table_ref[pl.ds(c0, TB), :], preferred_element_type=jnp.float32)
                acc_ref[pl.ds(r0, TB), :] += jnp.where(p < n, prod, 0.0)
            return carry

        lax.fori_loop(0, groups, body, 0)

    @pl.when(s > 0)
    def _():
        blk = out_ref.shape[0]
        r0 = pl.multiple_of((s - 1) * blk, blk)
        agg = acc_ref[pl.ds(r0, blk), :].astype(jnp.bfloat16)
        mixed = jnp.dot(agg, w_ref[...], preferred_element_type=jnp.float32)
        out_ref[...] = jnp.maximum(mixed, 0.0).astype(out_ref.dtype)


def local_tiles(order, rows, cols, counts, table, vals, adj, hub):
    n, width = table.shape
    const2 = lambda s, *_: (0, 0)
    const3 = lambda s, *_: (0, 0, 0)
    return pl.pallas_call(
        _local_kernel,
        grid_spec=pltpu.PrefetchScalarGridSpec(
            num_scalar_prefetch=4,
            grid=(1,),
            in_specs=[
                pl.BlockSpec((n, width), const2),
                pl.BlockSpec(vals.shape, const3),
                pl.BlockSpec(adj.shape, const2),
                pl.BlockSpec(hub.shape, const2),
            ],
            out_specs=pl.BlockSpec((n, width), const2),
        ),
        out_shape=jax.ShapeDtypeStruct((n, width), jnp.float32),
    )(order, rows, cols, counts, table, vals, adj, hub)


def remote_tiles(order, rows, cols, counts, table, vals, part, weight, lo):
    n, width = part.shape
    blk = 2048
    fin_steps = n // blk
    const2 = lambda s, *_: (0, 0)
    const3 = lambda s, *_: (0, 0, 0)
    fin = lambda s, *_: (jnp.maximum(s - 1, 0), 0)
    return pl.pallas_call(
        functools.partial(_remote_kernel, lo=lo),
        grid_spec=pltpu.PrefetchScalarGridSpec(
            num_scalar_prefetch=4,
            grid=(1 + fin_steps,),
            in_specs=[
                pl.BlockSpec(table.shape, const2),
                pl.BlockSpec(memory_space=pl.ANY),
                pl.BlockSpec((n, width), const2),
                pl.BlockSpec(weight.shape, const2),
            ],
            out_specs=pl.BlockSpec((blk, width), fin),
            scratch_shapes=[
                pltpu.VMEM(vals.shape, vals.dtype),
                pltpu.SemaphoreType.DMA((vals.shape[0] // GROUP,)),
            ],
        ),
        out_shape=jax.ShapeDtypeStruct((n, width), jnp.bfloat16),
    )(order, rows, cols, counts, table, vals, part, weight)


def slot_order(cols, count, width):
    slots = cols.shape[0]
    t = jnp.arange(slots, dtype=jnp.int32)
    live = t < count
    is_a = live & (cols < width)
    is_b = live & (cols >= width)
    dead = ~live
    n_a = jnp.sum(is_a.astype(jnp.int32))
    n_b = jnp.sum(is_b.astype(jnp.int32))
    pos = jnp.where(
        is_a,
        jnp.cumsum(is_a.astype(jnp.int32)) - 1,
        jnp.where(
            is_b,
            n_a + jnp.cumsum(is_b.astype(jnp.int32)) - 1,
            n_a + n_b + jnp.cumsum(dead.astype(jnp.int32)) - 1,
        ),
    )
    order = jnp.sum(jnp.where(pos[None, :] == t[:, None], t[None, :], 0), axis=1).astype(jnp.int32)
    return order, jnp.stack([n_a, n_b]).astype(jnp.int32)


def _gather_kernel(send_ref, feat_ref, out_ref, src_ref):
    n = feat_ref.shape[0]
    chunk = 512
    for i in range(n // chunk):
        sl = pl.ds(i * chunk, chunk)
        src_ref[sl, :] = feat_ref[sl, :].astype(jnp.float32)

    per_row = send_ref.shape[1]

    def body(g, carry):
        for h in range(per_row // 16):
            base = pl.multiple_of(g * per_row + h * 16, 16)
            rows = [src_ref[pl.ds(send_ref[g, h * 16 + k], 1), :] for k in range(16)]
            out_ref[pl.ds(base, 16), :] = jnp.concatenate(rows, axis=0).astype(out_ref.dtype)
        return carry

    lax.fori_loop(0, send_ref.shape[0], body, 0)


def gather_rows(send_idx, feat):
    n, width = feat.shape
    m = send_idx.shape[0] * send_idx.shape[1]
    return pl.pallas_call(
        _gather_kernel,
        grid_spec=pltpu.PrefetchScalarGridSpec(
            num_scalar_prefetch=1,
            grid=(1,),
            in_specs=[pl.BlockSpec((n, width), lambda s, *_: (0, 0))],
            out_specs=pl.BlockSpec((m, width), lambda s, *_: (0, 0)),
            scratch_shapes=[pltpu.VMEM((n, width), jnp.float32)],
        ),
        out_shape=jax.ShapeDtypeStruct((m, width), feat.dtype),
    )(send_idx, feat)


def per_device(
    features,
    hub_rows,
    hub_adjacency,
    tile_row,
    tile_col,
    tile_count,
    tile_values,
    send_rows,
    weight,
):
    local = features[0, 0]
    rows = local.shape[0]
    adjacency = hub_adjacency[0, 0]
    n_blk = lax.axis_size("blk")
    picks = hub_rows[0, 0][:, None] == jnp.arange(rows, dtype=jnp.int32)[None, :]
    hub_block = jnp.dot(
        picks.astype(local.dtype), local, preferred_element_type=jnp.float32
    ).astype(local.dtype)
    copies = jnp.broadcast_to(hub_block[None], (n_blk,) + hub_block.shape)
    hub_group = lax.all_to_all(copies, "blk", split_axis=0, concat_axis=0, tiled=True)
    hub_group = hub_group.reshape(-1, local.shape[-1])
    listing = send_rows[0, 0]
    outgoing = gather_rows(listing.reshape(-1, listing.shape[-1]), local)
    incoming = lax.all_to_all(outgoing, ("grp", "blk"), split_axis=0, concat_axis=0, tiled=True)
    t_rows = tile_row[0, 0]
    t_cols = tile_col[0, 0]
    vals = tile_values[0, 0]
    order, counts = slot_order(t_cols, tile_count[0, 0], rows // TB)
    part = local_tiles(order, t_rows, t_cols, counts, local, vals, adjacency, hub_group)
    out = remote_tiles(order, t_rows, t_cols, counts, incoming, vals, part, weight, rows // TB)
    return out[None, None]


def solution(mesh):
    return jax.shard_map(
        per_device,
        mesh=mesh,
        in_specs=(
            P("grp", "blk", None, None),
            P("grp", "blk", None),
            P("grp", "blk", None, None),
            P("grp", "blk", None),
            P("grp", "blk", None),
            P("grp", "blk"),
            P("grp", "blk", None, None, None),
            P("grp", "blk", None, None, None),
            P(),
        ),
        out_specs=P("grp", "blk", None, None),
        check_vma=False,
    )
```

```python
import functools

import jax
import jax.numpy as jnp
from jax import lax
from jax.experimental import pallas as pl
from jax.experimental.pallas import tpu as pltpu
from jax.sharding import PartitionSpec as P

TB = 128


GROUP = 16


def _slot_loop(order_ref, rows_ref, cols_ref, start, n, table_ref, vals_ref, acc_ref, lo):
    width = table_ref.shape[0] // TB

    def body(g, carry):
        for j in range(GROUP):
            p = g * GROUP + j
            t = order_ref[start + jnp.minimum(p, n - 1)]
            c = jnp.clip(cols_ref[t] - lo, 0, width - 1)
            r0 = pl.multiple_of(rows_ref[t] * TB, TB)
            c0 = pl.multiple_of(c * TB, TB)
            prod = jnp.dot(vals_ref[t], table_ref[pl.ds(c0, TB), :], preferred_element_type=jnp.float32)
            acc_ref[pl.ds(r0, TB), :] += jnp.where(p < n, prod, 0.0)
        return carry

    lax.fori_loop(0, (n + GROUP - 1) // GROUP, body, 0)


def _local_kernel(order_ref, rows_ref, cols_ref, counts_ref, table_ref, vals_ref, adj_ref, hub_ref,
                  acc_ref):
    n = acc_ref.shape[0]
    blk = 512
    for i in range(n // blk):
        sl = pl.ds(i * blk, blk)
        acc_ref[sl, :] = jnp.dot(adj_ref[sl, :], hub_ref[...], preferred_element_type=jnp.float32)
    _slot_loop(order_ref, rows_ref, cols_ref, 0, counts_ref[0], table_ref, vals_ref, acc_ref, 0)


def _remote_kernel(order_ref, rows_ref, cols_ref, counts_ref, table_ref, vals_hbm, acc_ref, w_ref,
                   out_ref, vbuf, sems, *, lo):
    s = pl.program_id(0)

    @pl.when(s == 0)
    def _():
        start = counts_ref[0]
        n = counts_ref[1]
        groups = (n + GROUP - 1) // GROUP
        width = table_ref.shape[0] // TB

        def issue(g):
            for j in range(GROUP):
                p = g * GROUP + j
                t = order_ref[start + jnp.minimum(p, n - 1)]
                pltpu.make_async_copy(vals_hbm.at[t], vbuf.at[p], sems.at[g]).start()

        @pl.when(groups > 0)
        def _():
            issue(0)

        def body(g, carry):
            @pl.when(g + 1 < groups)
            def _():
                issue(g + 1)

            base = pl.multiple_of(g * GROUP, GROUP)
            pltpu.make_async_copy(
                vals_hbm.at[pl.ds(0, GROUP)], vbuf.at[pl.ds(base, GROUP)], sems.at[g]
            ).wait()
            for j in range(GROUP):
                p = g * GROUP + j
                t = order_ref[start + jnp.minimum(p, n - 1)]
                c = jnp.clip(cols_ref[t] - lo, 0, width - 1)
                r0 = pl.multiple_of(rows_ref[t] * TB, TB)
                c0 = pl.multiple_of(c * TB, TB)
                prod = jnp.dot(vbuf[p], table_ref[pl.ds(c0, TB), :], preferred_element_type=jnp.float32)
                acc_ref[pl.ds(r0, TB), :] += jnp.where(p < n, prod, 0.0)
            return carry

        lax.fori_loop(0, groups, body, 0)

    @pl.when(s > 0)
    def _():
        blk = out_ref.shape[0]
        r0 = pl.multiple_of((s - 1) * blk, blk)
        agg = acc_ref[pl.ds(r0, blk), :].astype(jnp.bfloat16)
        mixed = jnp.dot(agg, w_ref[...], preferred_element_type=jnp.float32)
        out_ref[...] = jnp.maximum(mixed, 0.0).astype(out_ref.dtype)


def local_tiles(order, rows, cols, counts, table, vals, adj, hub):
    n, width = table.shape
    const2 = lambda s, *_: (0, 0)
    const3 = lambda s, *_: (0, 0, 0)
    return pl.pallas_call(
        _local_kernel,
        grid_spec=pltpu.PrefetchScalarGridSpec(
            num_scalar_prefetch=4,
            grid=(1,),
            in_specs=[
                pl.BlockSpec((n, width), const2),
                pl.BlockSpec(vals.shape, const3),
                pl.BlockSpec(adj.shape, const2),
                pl.BlockSpec(hub.shape, const2),
            ],
            out_specs=pl.BlockSpec((n, width), const2),
        ),
        out_shape=jax.ShapeDtypeStruct((n, width), jnp.float32),
    )(order, rows, cols, counts, table, vals, adj, hub)


def remote_tiles(order, rows, cols, counts, table, vals, part, weight, lo):
    n, width = part.shape
    blk = 1024
    fin_steps = n // blk
    const2 = lambda s, *_: (0, 0)
    const3 = lambda s, *_: (0, 0, 0)
    fin = lambda s, *_: (jnp.maximum(s - 1, 0), 0)
    return pl.pallas_call(
        functools.partial(_remote_kernel, lo=lo),
        grid_spec=pltpu.PrefetchScalarGridSpec(
            num_scalar_prefetch=4,
            grid=(1 + fin_steps,),
            in_specs=[
                pl.BlockSpec(table.shape, const2),
                pl.BlockSpec(memory_space=pl.ANY),
                pl.BlockSpec((n, width), const2),
                pl.BlockSpec(weight.shape, const2),
            ],
            out_specs=pl.BlockSpec((blk, width), fin),
            scratch_shapes=[
                pltpu.VMEM(vals.shape, vals.dtype),
                pltpu.SemaphoreType.DMA((vals.shape[0] // GROUP,)),
            ],
        ),
        out_shape=jax.ShapeDtypeStruct((n, width), jnp.bfloat16),
    )(order, rows, cols, counts, table, vals, part, weight)


def slot_order(cols, count, width):
    slots = cols.shape[0]
    t = jnp.arange(slots, dtype=jnp.int32)
    live = t < count
    is_a = live & (cols < width)
    is_b = live & (cols >= width)
    dead = ~live
    n_a = jnp.sum(is_a.astype(jnp.int32))
    n_b = jnp.sum(is_b.astype(jnp.int32))
    pos = jnp.where(
        is_a,
        jnp.cumsum(is_a.astype(jnp.int32)) - 1,
        jnp.where(
            is_b,
            n_a + jnp.cumsum(is_b.astype(jnp.int32)) - 1,
            n_a + n_b + jnp.cumsum(dead.astype(jnp.int32)) - 1,
        ),
    )
    order = jnp.sum(jnp.where(pos[None, :] == t[:, None], t[None, :], 0), axis=1).astype(jnp.int32)
    return order, jnp.stack([n_a, n_b]).astype(jnp.int32)


def _gather_kernel(send_ref, feat_ref, out_ref, src_ref):
    n = feat_ref.shape[0]
    chunk = 512
    for i in range(n // chunk):
        sl = pl.ds(i * chunk, chunk)
        src_ref[sl, :] = feat_ref[sl, :].astype(jnp.float32)

    per_row = send_ref.shape[1]

    def body(g, carry):
        for h in range(per_row // 16):
            base = pl.multiple_of(g * per_row + h * 16, 16)
            rows = [src_ref[pl.ds(send_ref[g, h * 16 + k], 1), :] for k in range(16)]
            out_ref[pl.ds(base, 16), :] = jnp.concatenate(rows, axis=0).astype(out_ref.dtype)
        return carry

    lax.fori_loop(0, send_ref.shape[0], body, 0)


def gather_rows(send_idx, feat):
    n, width = feat.shape
    m = send_idx.shape[0] * send_idx.shape[1]
    return pl.pallas_call(
        _gather_kernel,
        grid_spec=pltpu.PrefetchScalarGridSpec(
            num_scalar_prefetch=1,
            grid=(1,),
            in_specs=[pl.BlockSpec((n, width), lambda s, *_: (0, 0))],
            out_specs=pl.BlockSpec((m, width), lambda s, *_: (0, 0)),
            scratch_shapes=[pltpu.VMEM((n, width), jnp.float32)],
        ),
        out_shape=jax.ShapeDtypeStruct((m, width), feat.dtype),
    )(send_idx, feat)


def per_device(
    features,
    hub_rows,
    hub_adjacency,
    tile_row,
    tile_col,
    tile_count,
    tile_values,
    send_rows,
    weight,
):
    local = features[0, 0]
    rows = local.shape[0]
    adjacency = hub_adjacency[0, 0]
    n_blk = lax.axis_size("blk")
    picks = hub_rows[0, 0][:, None] == jnp.arange(rows, dtype=jnp.int32)[None, :]
    hub_block = jnp.dot(
        picks.astype(local.dtype), local, preferred_element_type=jnp.float32
    ).astype(local.dtype)
    copies = jnp.broadcast_to(hub_block[None], (n_blk,) + hub_block.shape)
    hub_group = lax.all_to_all(copies, "blk", split_axis=0, concat_axis=0, tiled=True)
    hub_group = hub_group.reshape(-1, local.shape[-1])
    listing = send_rows[0, 0]
    outgoing = gather_rows(listing.reshape(-1, listing.shape[-1]), local)
    incoming = lax.all_to_all(outgoing, ("grp", "blk"), split_axis=0, concat_axis=0, tiled=True)
    t_rows = tile_row[0, 0]
    t_cols = tile_col[0, 0]
    vals = tile_values[0, 0]
    order, counts = slot_order(t_cols, tile_count[0, 0], rows // TB)
    part = local_tiles(order, t_rows, t_cols, counts, local, vals, adjacency, hub_group)
    out = remote_tiles(order, t_rows, t_cols, counts, incoming, vals, part, weight, rows // TB)
    return out[None, None]


def solution(mesh):
    return jax.shard_map(
        per_device,
        mesh=mesh,
        in_specs=(
            P("grp", "blk", None, None),
            P("grp", "blk", None),
            P("grp", "blk", None, None),
            P("grp", "blk", None),
            P("grp", "blk", None),
            P("grp", "blk"),
            P("grp", "blk", None, None, None),
            P("grp", "blk", None, None, None),
            P(),
        ),
        out_specs=P("grp", "blk", None, None),
        check_vma=False,
    )
```
